32 devices in a mesh: section: 4 (over z), dp: 2 (over x), tensor: 4 (over y, core).
Axes of the slice: x: 2, y: 2, z: 4, core: 2. Of those that a mesh axis runs over, the one named last changes fastest.
Arguments:
- hidden: bfloat16 [4, 2, 256, 16384], P('section', 'dp', None, 'tensor'), may hold values from -80 to 80
- owner: int32 [4, 2, 256, 1], P('section', 'dp'), may hold values from 0 to 1; in each aligned block of 256 rows (0 to 255, 256 to 511, ..., all dimensions but the last counted through in order) at most 192 rows name the same one
- start: int32 [4, 2], P('section', 'dp'), may hold values from 0 to 1792
- live: int32 [4, 2], P('section', 'dp'), may hold values from 128 to 256
- norm_gain: float32 [4, 16384], P('section', 'tensor'), may hold values from 0.5 to 1.5
- w_kv: bfloat16 [4, 16384, 2048], P('section', 'tensor'), may hold values from -0.046875 to 0.046875
Outputs:
- kv_cache: bfloat16 [4, 2, 384, 2048], P('section', 'dp', None, 'tensor')
The draws below stay inside these ranges and needn't reach their ends.
Inputs may be any that keep to these rules, and one draw needn't show every extreme that they name: `owner`: among the 256 rows of one block no group is named by more than 192 rows, and some block names one group exactly 192 times. The live rows of a block are its first ones.
All inputs are finite; a program needn't handle non-finite values.
Results may differ from the reference program's by a relative error of at most 0.0049.
Values may be sent and summed in bfloat16 or wider, within the bound.
No kernel may reach another device: no remote copies, remote signals or barrier semaphores. Data moves between devices by JAX's collectives and lax.ppermute only.
A program may use at most 64 MiB of HBM per device.

```python
import math
import jax
import jax.numpy as jnp
import numpy as np
from jax import lax

D = 16384
KVH = 8
HD = 128
PROMPT = 2048
TOK = 256
CAP = 192
SLOTS = 384
KVC = 2048
N_SECTION = 4
N_DP = 2


def draw_hidden(key, part):
    key_noise, key_rows, key_cols = jax.random.split(jax.random.fold_in(key, 11), 3)
    shape = (N_SECTION, N_DP, TOK, D)
    feature = jnp.arange(D, dtype=jnp.float32) / D
    col_scale = jnp.exp(jax.random.uniform(key_cols, (D,), jnp.float32, 0.0, math.log(2.5)))
    noise = jnp.clip(jax.random.normal(key_noise, shape, jnp.float32), -4.0, 4.0)
    rising = 3.0 ** feature
    row_scale = jnp.exp(jax.random.uniform(key_rows, (N_SECTION, N_DP, TOK, 1), jnp.float32, math.log(0.5), math.log(2.0)))
    return jnp.clip(noise * rising * col_scale * row_scale, -80.0, 80.0).astype(jnp.bfloat16)


def touch_ends(drawn, rng, low, largest):
    index_at = [jax.random.randint(jax.random.fold_in(rng, axis), (), 0, length) for axis, length in enumerate(drawn.shape)]
    main_axis = drawn.shape.index(max(drawn.shape))
    next_to = index_at[:main_axis] + [(index_at[main_axis] + 1) % drawn.shape[main_axis]] + index_at[main_axis + 1:]
    return drawn.at[tuple(index_at)].set(low).at[tuple(next_to)].set(largest)


def shard_levels(rng, shape, cuts, low, top_value):
    gain, own = 1.0, jax.random.fold_in(rng, 6)
    for dim, parts in cuts:
        steps = jnp.exp(jax.random.uniform(jax.random.fold_in(own, dim), (parts,), jnp.float32, low / len(cuts), top_value / len(cuts)))
        gain = gain * jnp.repeat(steps, shape[dim] // parts).reshape([-1 if axis == dim else 1 for axis in range(len(shape))])
    return gain


def shared_out(own_key, own, number, rows, number_of, top, most, skew):
    sequence = jax.random.permutation(own_key, number_of)
    packed, ordinary = shares(number_of, rows * top, most, skew, True), shares(number_of, rows * top, most, skew, False)
    places = jnp.arange(number_of)

    def named(lengths, turn):
        used = int((lengths > 0).sum())
        fixed = max(1, used // 4)
        passed = fixed + (places - fixed + turn * (used - fixed)) % max(1, number_of - fixed)
        return jnp.zeros((number_of,), jnp.int32).at[sequence[jnp.where(places < fixed, places, passed)]].set(jnp.asarray(lengths, jnp.int32))

    lengths = jnp.where(number % 4 == 0, named(packed, number // 4), named(ordinary, number - number // 4 - 1))
    mixed = jax.random.permutation(jax.random.fold_in(own, 3), number_of)
    giver, receiver = mixed[0:number_of // 2 * 2:2], mixed[1:number_of // 2 * 2:2]
    room = jnp.minimum(lengths[giver] - 1, most - lengths[receiver]) // 2
    room = jnp.where((giver == sequence[0]) | (receiver == sequence[0]) | (lengths[receiver] == 0), 0, jnp.maximum(room, 0))
    passed = jax.random.randint(jax.random.fold_in(own, 4), (number_of // 2,), 0, 1 << 20) % (room + 1)
    lengths = lengths.at[giver].add(-passed).at[receiver].add(passed)
    members = jnp.searchsorted(jnp.cumsum(lengths), jnp.arange(rows * top), side="right").astype(jnp.int32)
    grid = members.reshape(top, rows).T
    grid = grid[jax.random.permutation(jax.random.fold_in(own, 1), rows)]
    turn = jax.random.randint(jax.random.fold_in(own, 2), (rows, 1), 0, top)
    return jnp.take_along_axis(grid, (jnp.arange(top)[None, :] + turn) % top, axis=1)


def shares(count, total, bound, skew, full):
    portions = [(1 << 20) // math.isqrt(standing ** skew) + 1 for standing in range(1, count + 1)]
    largest = bound if full else min(bound, max(-(-total // count), total * portions[0] // sum(portions)))
    least = 1 if total - largest >= count - 1 else 0
    holding, surplus = [largest] + [least] * (count - 1), total - largest - least * (count - 1)
    while surplus > 0:
        free = [i for i in range(1, count) if holding[i] < largest] or [i for i in range(1, count) if holding[i] < bound]
        whole, remaining = sum([portions[i] for i in free]), surplus
        for i in free:
            more = min(bound - holding[i], max(1, remaining * portions[i] // whole), surplus)
            holding[i] = holding[i] + more
            surplus = surplus - more
    return np.array(holding)


def centred(key, shape, scale, reach, cuts=(), held_as=jnp.bfloat16):
    gain = shard_levels(key, shape, cuts, -0.22, 0.18) if cuts else 1.0
    drawn = jax.random.normal(key, shape, jnp.float32) * scale * gain
    return jnp.minimum(jnp.maximum(drawn, -reach), reach).astype(held_as)


def setup_inputs(seed: int = 0) -> dict:
    key_list = jax.random.split(jax.random.key(seed), 7)
    hidden = draw_hidden(jax.random.fold_in(key_list[6], 71), 0)
    owner_keys = jax.random.split(jax.random.fold_in(key_list[1], 1), N_SECTION * N_DP * TOK // TOK)
    owner_turns = jax.random.permutation(jax.random.fold_in(key_list[1], 3), N_SECTION * N_DP * TOK // TOK)
    owner = jax.vmap(lambda own, number: shared_out(jax.random.fold_in(key_list[1], 2), own, number, TOK, N_DP, 1, CAP, 2))(owner_keys, owner_turns).reshape((N_SECTION, N_DP, TOK, 1))
    start = touch_ends(jax.random.randint(key_list[2], (N_SECTION, N_DP), 0, PROMPT - TOK + 1), jax.random.fold_in(key_list[2], 1), 0, PROMPT - TOK).astype(jnp.int32)
    live = touch_ends(jax.random.randint(key_list[3], (N_SECTION, N_DP), TOK // 2, TOK + 1), jax.random.fold_in(key_list[3], 1), TOK // 2, TOK).astype(jnp.int32)
    norm_gain = jnp.clip(1.0 + 0.1 * jax.random.normal(key_list[4], (N_SECTION, D), jnp.float32), 0.5, 1.5)
    w_kv = centred(key_list[5], (N_SECTION, D, KVC), D ** -0.5, 0.046875, ((0, 4), (1, 4)))
    return {"hidden": hidden, "owner": owner, "start": start, "live": live, "norm_gain": norm_gain, "w_kv": w_kv}


EPSILON = 1e-05
ROPE_BASE = 500000.0

def rope_keys(kv_rows, positions):
    half_size = HD // 2
    inverse = ROPE_BASE ** (-(jnp.arange(half_size, dtype=jnp.float32) * 2.0 / HD))
    angles = positions.astype(jnp.float32)[:, None] * inverse[None, :]
    cosines = jnp.cos(angles)[:, None, :]
    sines = jnp.sin(angles)[:, None, :]
    key_part = kv_rows[:, :, 0, :]
    front_half = key_part[..., :half_size]
    back_half = key_part[..., half_size:]
    rotated = jnp.concatenate([front_half * cosines - back_half * sines, back_half * cosines + front_half * sines], axis=-1)
    return jnp.stack([rotated, kv_rows[:, :, 1, :]], axis=2)

def rank_in_group(target, row_alive):
    onehot = ((target[:, None] == jnp.arange(N_DP, dtype=jnp.int32)[None, :]) & row_alive[:, None]).astype(jnp.int32)
    earlier_hits = jnp.cumsum(onehot, axis=0).astype(jnp.int32) - onehot
    return lax.optimization_barrier(jnp.sum(earlier_hits * onehot, axis=1)).astype(jnp.int32)

def reference(hidden, owner, start, live, norm_gain, w_kv):

    def one_section(section_idx):
        earlier = jnp.maximum(section_idx - 1, 0).astype(jnp.int32)
        tok_rows = hidden[earlier]
        widened = tok_rows.astype(jnp.float32)
        mean_sq = lax.optimization_barrier(jnp.mean(widened * widened, axis=-1, keepdims=True))
        normed = (widened * norm_gain[section_idx] * lax.rsqrt(mean_sq + EPSILON)).astype(jnp.bfloat16)
        kv_rows = jnp.dot(normed.reshape(N_DP * TOK, D), w_kv[section_idx], preferred_element_type=jnp.float32)
        row_index = jnp.arange(TOK, dtype=jnp.int32)
        positions = (start[earlier][:, None] + row_index[None, :]).reshape(-1).astype(jnp.int32)
        kv_rows = rope_keys(kv_rows.reshape(N_DP * TOK, KVH, 2, HD), positions)
        kv_rows = kv_rows.reshape(N_DP * TOK, KVC).astype(jnp.bfloat16)
        target = owner[earlier][:, :, 0].astype(jnp.int32)
        row_alive = row_index[None, :] < live[earlier][:, None]
        rank_in = jax.vmap(rank_in_group)(target, row_alive)
        target_group = jnp.where(row_alive, target, N_DP).astype(jnp.int32)
        target_slot = (jnp.arange(N_DP, dtype=jnp.int32)[:, None] * CAP + rank_in).astype(jnp.int32)
        sectioned = jnp.zeros((N_DP, SLOTS, KVC), jnp.bfloat16)
        sectioned = sectioned.at[target_group.reshape(-1), target_slot.reshape(-1)].set(kv_rows, mode='drop')
        return jnp.where(section_idx > 0, sectioned, jnp.zeros_like(sectioned))
    return lax.map(one_section, jnp.arange(N_SECTION, dtype=jnp.int32))
```

```python
import jax
import jax.numpy as jnp
from jax import lax
from jax.sharding import PartitionSpec as P

D = 16384
HD = 128


EPSILON = 1e-05
ROPE_BASE = 500000.0
CHUNKS = 4


def shifted(block, axis, distance):
    devices = range(lax.axis_size(axis))
    route = [(i - distance, i) for i in devices if i - distance in devices]
    return lax.ppermute(block, axis, route)


def rotate_keys(kv_rows, positions):
    half_size = kv_rows.shape[3] // 2
    head_size = kv_rows.shape[3]
    inverse = ROPE_BASE ** (-(jnp.arange(half_size, dtype=jnp.float32) * 2.0 / head_size))
    angles = positions.astype(jnp.float32)[:, None] * inverse[None, :]
    cosines = jnp.cos(angles)[:, None, :]
    sines = jnp.sin(angles)[:, None, :]
    key_part = kv_rows[:, :, 0, :]
    front_half = key_part[..., :half_size]
    back_half = key_part[..., half_size:]
    rotated = jnp.concatenate(
        [front_half * cosines - back_half * sines, back_half * cosines + front_half * sines],
        axis=-1,
    )
    return jnp.stack([rotated, kv_rows[:, :, 1, :]], axis=2)


def per_device(hidden, owner, start, live, norm_gain, w_kv):
    groups = lax.axis_size("dp")
    tok_count = hidden.shape[2]
    capacity = 3 * tok_count // (2 * groups)
    slot_count = capacity * groups

    tok_rows = hidden[0, 0]
    target = owner[0, 0, :, 0]
    row_index = jnp.arange(tok_count, dtype=jnp.int32)
    row_alive = row_index < live[0, 0]
    onehot = (
        (target[:, None] == jnp.arange(groups, dtype=jnp.int32)[None, :]) & row_alive[:, None]
    ).astype(jnp.int32)
    row_rank = jnp.sum((jnp.cumsum(onehot, axis=0) - onehot) * onehot, axis=1)
    row_slot = jnp.where(row_alive, target * capacity + row_rank, slot_count)
    position = start[0, 0] + row_index
    widened = tok_rows.astype(jnp.float32)
    sum_sq = lax.psum(jnp.sum(widened * widened, axis=1), "tensor")
    meta = jnp.stack([row_slot, position])
    meta, sum_sq = shifted((meta, sum_sq), "section", 1)

    first = lax.axis_index("section") == 0
    row_slot = jnp.where(first, slot_count, meta[0])
    position = meta[1]
    scale = lax.rsqrt(sum_sq / D + EPSILON)
    gain = norm_gain[0]
    weight = w_kv[0]
    step = tok_count // CHUNKS
    pieces = []
    for k in range(CHUNKS):
        rows = slice(k * step, (k + 1) * step)
        arrived = shifted(tok_rows[rows], "section", 1)
        normed = (arrived.astype(jnp.float32) * gain * scale[rows][:, None]).astype(jnp.bfloat16)
        partial = jnp.dot(normed, weight, preferred_element_type=jnp.float32)
        pieces.append(
            lax.psum_scatter(partial, "tensor", scatter_dimension=1, tiled=True)
        )
    summed = jnp.concatenate(pieces, axis=0)
    local_cols = summed.shape[1]
    local_kv = summed.reshape(tok_count, local_cols // (2 * HD), 2, HD)
    result = rotate_keys(local_kv, position).reshape(tok_count, local_cols).astype(jnp.bfloat16)

    placing = row_slot[None, :] == jnp.arange(slot_count, dtype=jnp.int32)[:, None]
    packed = jnp.dot(
        placing.astype(jnp.bfloat16), result, preferred_element_type=jnp.float32
    ).astype(jnp.bfloat16)
    packed = packed.reshape(groups, capacity, local_cols)
    routed = lax.all_to_all(packed, "dp", split_axis=0, concat_axis=0, tiled=True)
    return routed.reshape(1, 1, slot_count, local_cols)


def solution(mesh):
    in_specs = (
        P("section", "dp", None, "tensor"),
        P("section", "dp", None, None),
        P("section", "dp"),
        P("section", "dp"),
        P("section", "tensor"),
        P("section", "tensor", None),
    )
    out_specs = P("section", "dp", None, "tensor")
    return jax.shard_map(
        per_device, mesh=mesh, in_specs=in_specs, out_specs=out_specs, check_vma=False
    )
```

```python
import jax
import jax.numpy as jnp
from jax import lax
from jax.sharding import PartitionSpec as P

D = 16384
HD = 128


EPSILON = 1e-05
ROPE_BASE = 500000.0
CHUNKS = 4


def shifted(block, axis, distance):
    devices = range(lax.axis_size(axis))
    route = [(i - distance, i) for i in devices if i - distance in devices]
    return lax.ppermute(block, axis, route)


def scatter_sum(partial, axis):
    size = lax.axis_size(axis)
    me = lax.axis_index(axis)
    rows, width = partial.shape
    block = width // size
    current = partial.reshape(rows, size, block)
    bit = 1
    while bit < size:
        halves = current.reshape(rows, -1, 2, block)
        mine_hi = (me // bit) % 2 == 1
        keep = jnp.where(mine_hi, halves[:, :, 1], halves[:, :, 0])
        send = jnp.where(mine_hi, halves[:, :, 0], halves[:, :, 1])
        pairs = [(i, i ^ bit) for i in range(size)]
        current = (keep + lax.ppermute(send, axis, pairs)).reshape(rows, -1, block)
        bit *= 2
    return current.reshape(rows, block)


def rotate_keys(kv_rows, positions):
    half_size = kv_rows.shape[3] // 2
    head_size = kv_rows.shape[3]
    inverse = ROPE_BASE ** (-(jnp.arange(half_size, dtype=jnp.float32) * 2.0 / head_size))
    angles = positions.astype(jnp.float32)[:, None] * inverse[None, :]
    cosines = jnp.cos(angles)[:, None, :]
    sines = jnp.sin(angles)[:, None, :]
    key_part = kv_rows[:, :, 0, :]
    front_half = key_part[..., :half_size]
    back_half = key_part[..., half_size:]
    rotated = jnp.concatenate(
        [front_half * cosines - back_half * sines, back_half * cosines + front_half * sines],
        axis=-1,
    )
    return jnp.stack([rotated, kv_rows[:, :, 1, :]], axis=2)


def per_device(hidden, owner, start, live, norm_gain, w_kv):
    groups = lax.axis_size("dp")
    tok_count = hidden.shape[2]
    capacity = 3 * tok_count // (2 * groups)
    slot_count = capacity * groups

    tok_rows = hidden[0, 0]
    target = owner[0, 0, :, 0]
    row_index = jnp.arange(tok_count, dtype=jnp.int32)
    row_alive = row_index < live[0, 0]
    onehot = (
        (target[:, None] == jnp.arange(groups, dtype=jnp.int32)[None, :]) & row_alive[:, None]
    ).astype(jnp.int32)
    row_rank = jnp.sum((jnp.cumsum(onehot, axis=0) - onehot) * onehot, axis=1)
    row_slot = jnp.where(row_alive, target * capacity + row_rank, slot_count)
    position = start[0, 0] + row_index
    widened = tok_rows.astype(jnp.float32)
    sum_sq = lax.psum(jnp.sum(widened * widened, axis=1), "tensor")
    meta = jnp.stack([row_slot, position])
    meta, sum_sq = shifted((meta, sum_sq), "section", 1)

    first = lax.axis_index("section") == 0
    row_slot = jnp.where(first, slot_count, meta[0])
    position = meta[1]
    scale = lax.rsqrt(sum_sq / D + EPSILON)
    gain = norm_gain[0]
    weight = w_kv[0]
    local_width = tok_rows.shape[1]
    step = local_width // CHUNKS
    partial = None
    for k in range(CHUNKS):
        cols = slice(k * step, (k + 1) * step)
        arrived = shifted(tok_rows[:, cols], "section", 1)
        normed = (arrived.astype(jnp.float32) * gain[cols] * scale[:, None]).astype(jnp.bfloat16)
        term = jnp.dot(normed, weight[cols], preferred_element_type=jnp.float32)
        partial = term if partial is None else partial + term
    summed = scatter_sum(partial, "tensor")
    local_cols = summed.shape[1]
    local_kv = summed.reshape(tok_count, local_cols // (2 * HD), 2, HD)
    result = rotate_keys(local_kv, position).reshape(tok_count, local_cols).astype(jnp.bfloat16)

    placing = row_slot[None, :] == jnp.arange(slot_count, dtype=jnp.int32)[:, None]
    packed = jnp.dot(
        placing.astype(jnp.bfloat16), result, preferred_element_type=jnp.float32
    ).astype(jnp.bfloat16)
    packed = packed.reshape(groups, capacity, local_cols)
    routed = lax.all_to_all(packed, "dp", split_axis=0, concat_axis=0, tiled=True)
    return routed.reshape(1, 1, slot_count, local_cols)


def solution(mesh):
    in_specs = (
        P("section", "dp", None, "tensor"),
        P("section", "dp", None, None),
        P("section", "dp"),
        P("section", "dp"),
        P("section", "tensor"),
        P("section", "tensor", None),
    )
    out_specs = P("section", "dp", None, "tensor")
    return jax.shard_map(
        per_device, mesh=mesh, in_specs=in_specs, out_specs=out_specs, check_vma=False
    )
```

```python
import jax
import jax.numpy as jnp
from jax import lax
from jax.sharding import PartitionSpec as P

D = 16384
HD = 128


EPSILON = 1e-05
ROPE_BASE = 500000.0
CHUNKS = 4


def shifted(block, axis, distance):
    devices = range(lax.axis_size(axis))
    route = [(i - distance, i) for i in devices if i - distance in devices]
    return lax.ppermute(block, axis, route)


def scatter_sum(partial, axis):
    size = lax.axis_size(axis)
    me = lax.axis_index(axis)
    levels = size.bit_length() - 1
    width, rows = partial.shape
    current = partial.reshape((2,) * levels + (width // size, rows))
    bit = 1
    while bit < size:
        mine = (me // bit) % 2
        where = current.ndim - 3
        keep = lax.dynamic_index_in_dim(current, mine, where, keepdims=False)
        send = lax.dynamic_index_in_dim(current, 1 - mine, where, keepdims=False)
        pairs = [(i, i ^ bit) for i in range(size)]
        current = keep + lax.ppermute(send, axis, pairs)
        bit *= 2
    return current


def rotate_keys(kv_cols, positions):
    head_size = kv_cols.shape[2]
    half_size = head_size // 2
    inverse = ROPE_BASE ** (-(jnp.arange(half_size, dtype=jnp.float32) * 2.0 / head_size))
    angles = inverse[:, None] * positions.astype(jnp.float32)[None, :]
    cosines = jnp.cos(angles)[None]
    sines = jnp.sin(angles)[None]
    key_part = kv_cols[:, 0]
    front_half = key_part[:, :half_size]
    back_half = key_part[:, half_size:]
    rotated = jnp.concatenate(
        [front_half * cosines - back_half * sines, back_half * cosines + front_half * sines],
        axis=1,
    )
    return jnp.stack([rotated, kv_cols[:, 1]], axis=1)


def per_device(hidden, owner, start, live, norm_gain, w_kv):
    groups = lax.axis_size("dp")
    tok_count = hidden.shape[2]
    capacity = 3 * tok_count // (2 * groups)
    slot_count = capacity * groups

    tok_rows = hidden[0, 0]
    target = owner[0, 0, :, 0]
    row_index = jnp.arange(tok_count, dtype=jnp.int32)
    row_alive = row_index < live[0, 0]
    onehot = (
        (target[:, None] == jnp.arange(groups, dtype=jnp.int32)[None, :]) & row_alive[:, None]
    ).astype(jnp.int32)
    row_rank = jnp.sum((jnp.cumsum(onehot, axis=0) - onehot) * onehot, axis=1)
    row_slot = jnp.where(row_alive, target * capacity + row_rank, slot_count)
    position = start[0, 0] + row_index
    widened = tok_rows.astype(jnp.float32)
    sum_sq = lax.psum(jnp.sum(widened * widened, axis=1), "tensor")
    meta = jnp.stack([sum_sq, row_slot.astype(jnp.float32), position.astype(jnp.float32)])
    meta = shifted(meta, "section", 1)
    sum_sq = meta[0]

    first = lax.axis_index("section") == 0
    row_slot = jnp.where(first, slot_count, meta[1].astype(jnp.int32))
    position = meta[2].astype(jnp.int32)
    scale = lax.rsqrt(sum_sq / D + EPSILON)
    gain = norm_gain[0]
    weight = w_kv[0]
    local_width = tok_rows.shape[1]
    step = local_width // CHUNKS
    partial = None
    for k in range(CHUNKS):
        cols = slice(k * step, (k + 1) * step)
        arrived = shifted(tok_rows[:, cols], "section", 1)
        normed = (arrived.astype(jnp.float32) * gain[cols] * scale[:, None]).astype(jnp.bfloat16)
        term = lax.dot_general(
            weight[cols], normed, (((0,), (1,)), ((), ())), preferred_element_type=jnp.float32
        )
        partial = term if partial is None else partial + term
    summed = scatter_sum(partial, "tensor")
    local_cols = summed.shape[0]
    local_kv = summed.reshape(local_cols // (2 * HD), 2, HD, tok_count)
    result = rotate_keys(local_kv, position).reshape(local_cols, tok_count).astype(jnp.bfloat16)

    placing = row_slot[None, :] == jnp.arange(slot_count, dtype=jnp.int32)[:, None]
    packed = lax.dot_general(
        placing.astype(jnp.bfloat16), result, (((1,), (1,)), ((), ())),
        preferred_element_type=jnp.float32,
    ).astype(jnp.bfloat16)
    packed = packed.reshape(groups, capacity, local_cols)
    me = lax.axis_index("dp")
    received = [None] * groups
    received[0] = lax.dynamic_index_in_dim(packed, me, 0, keepdims=False)
    for offset in range(1, groups):
        outgoing = lax.dynamic_index_in_dim(packed, (me + offset) % groups, 0, keepdims=False)
        pairs = [(i, (i + offset) % groups) for i in range(groups)]
        received[offset] = lax.ppermute(outgoing, "dp", pairs)
    stacked = jnp.stack(received)
    routed = jnp.take(stacked, (me - jnp.arange(groups, dtype=jnp.int32)) % groups, axis=0)
    return routed.reshape(1, 1, slot_count, local_cols)


def solution(mesh):
    in_specs = (
        P("section", "dp", None, "tensor"),
        P("section", "dp", None, None),
        P("section", "dp"),
        P("section", "dp"),
        P("section", "tensor"),
        P("section", "tensor", None),
    )
    out_specs = P("section", "dp", None, "tensor")
    return jax.shard_map(
        per_device, mesh=mesh, in_specs=in_specs, out_specs=out_specs, check_vma=False
    )
```

```python
import jax
import jax.numpy as jnp
from jax import lax
from jax.sharding import PartitionSpec as P

D = 16384
HD = 128


EPSILON = 1e-05
ROPE_BASE = 500000.0
CHUNKS = 4


def shifted(block, axis, distance):
    devices = range(lax.axis_size(axis))
    route = [(i - distance, i) for i in devices if i - distance in devices]
    return lax.ppermute(block, axis, route)


def scatter_sum(blocks, axis):
    size = lax.axis_size(axis)
    current = blocks
    bit = 1
    while bit < size:
        half = current.shape[0] // 2
        keep, send = current[:half], current[half:]
        if bit >= 2:
            send = send.astype(jnp.bfloat16)
        pairs = [(i, i ^ bit) for i in range(size)]
        current = keep + lax.ppermute(send, axis, pairs).astype(jnp.float32)
        bit *= 2
    return current[0]


def bit_reversed(index, levels):
    return int(format(index, "0%db" % levels)[::-1], 2) if levels else 0


def rotate_keys(kv_cols, positions):
    head_size = kv_cols.shape[2]
    half_size = head_size // 2
    inverse = ROPE_BASE ** (-(jnp.arange(half_size, dtype=jnp.float32) * 2.0 / head_size))
    angles = inverse[:, None] * positions.astype(jnp.float32)[None, :]
    cosines = jnp.cos(angles)[None]
    sines = jnp.sin(angles)[None]
    key_part = kv_cols[:, 0]
    front_half = key_part[:, :half_size]
    back_half = key_part[:, half_size:]
    rotated = jnp.concatenate(
        [front_half * cosines - back_half * sines, back_half * cosines + front_half * sines],
        axis=1,
    )
    return jnp.stack([rotated, kv_cols[:, 1]], axis=1)


def per_device(hidden, owner, start, live, norm_gain, w_kv):
    groups = lax.axis_size("dp")
    tok_count = hidden.shape[2]
    capacity = 3 * tok_count // (2 * groups)
    slot_count = capacity * groups

    tok_rows = hidden[0, 0]
    target = owner[0, 0, :, 0]
    row_index = jnp.arange(tok_count, dtype=jnp.int32)
    row_alive = row_index < live[0, 0]
    onehot = (
        (target[:, None] == jnp.arange(groups, dtype=jnp.int32)[None, :]) & row_alive[:, None]
    ).astype(jnp.int32)
    row_rank = jnp.sum((jnp.cumsum(onehot, axis=0) - onehot) * onehot, axis=1)
    row_slot = jnp.where(row_alive, target * capacity + row_rank, slot_count)
    position = start[0, 0] + row_index
    widened = tok_rows.astype(jnp.float32)
    sum_sq = lax.psum(jnp.sum(widened * widened, axis=1), "tensor")
    meta = jnp.stack([sum_sq, row_slot.astype(jnp.float32), position.astype(jnp.float32)])
    meta = shifted(meta, "section", 1)
    sum_sq = meta[0]

    first = lax.axis_index("section") == 0
    row_slot = jnp.where(first, slot_count, meta[1].astype(jnp.int32))
    position = meta[2].astype(jnp.int32)
    scale = lax.rsqrt(sum_sq / D + EPSILON)
    gain = norm_gain[0]
    weight = w_kv[0]
    local_width = tok_rows.shape[1]
    step = local_width // CHUNKS
    tensor = lax.axis_size("tensor")
    me_t = lax.axis_index("tensor")
    levels = tensor.bit_length() - 1
    block = weight.shape[1] // tensor
    partial = None
    for k in range(CHUNKS):
        cols = slice(k * step, (k + 1) * step)
        arrived = shifted(tok_rows[:, cols], "section", 1)
        normed = (arrived.astype(jnp.float32) * gain[cols] * scale[:, None]).astype(jnp.bfloat16)
        terms = []
        for s in range(tensor):
            column = jnp.bitwise_xor(me_t, bit_reversed(s, levels)) * block
            piece = lax.dynamic_slice_in_dim(weight[cols], column, block, axis=1)
            terms.append(
                lax.dot_general(
                    piece, normed, (((0,), (1,)), ((), ())), preferred_element_type=jnp.float32
                )
            )
        term = jnp.stack(terms)
        partial = term if partial is None else partial + term
    summed = scatter_sum(partial, "tensor")
    local_cols = summed.shape[0]
    local_kv = summed.reshape(local_cols // (2 * HD), 2, HD, tok_count)
    result = rotate_keys(local_kv, position).reshape(local_cols, tok_count).astype(jnp.bfloat16)

    placing = row_slot[None, :] == jnp.arange(slot_count, dtype=jnp.int32)[:, None]
    packed = lax.dot_general(
        placing.astype(jnp.bfloat16), result, (((1,), (1,)), ((), ())),
        preferred_element_type=jnp.float32,
    ).astype(jnp.bfloat16)
    packed = packed.reshape(groups, capacity, local_cols)
    me = lax.axis_index("dp")
    received = [None] * groups
    received[0] = lax.dynamic_index_in_dim(packed, me, 0, keepdims=False)
    for offset in range(1, groups):
        outgoing = lax.dynamic_index_in_dim(packed, (me + offset) % groups, 0, keepdims=False)
        pairs = [(i, (i + offset) % groups) for i in range(groups)]
        received[offset] = lax.ppermute(outgoing, "dp", pairs)
    stacked = jnp.stack(received)
    routed = jnp.take(stacked, (me - jnp.arange(groups, dtype=jnp.int32)) % groups, axis=0)
    return routed.reshape(1, 1, slot_count, local_cols)


def solution(mesh):
    in_specs = (
        P("section", "dp", None, "tensor"),
        P("section", "dp", None, None),
        P("section", "dp"),
        P("section", "dp"),
        P("section", "tensor"),
        P("section", "tensor", None),
    )
    out_specs = P("section", "dp", None, "tensor")
    return jax.shard_map(
        per_device, mesh=mesh, in_specs=in_specs, out_specs=out_specs, check_vma=False
    )
```

```python
import jax
import jax.numpy as jnp
from jax import lax
from jax.sharding import PartitionSpec as P

D = 16384
HD = 128


EPSILON = 1e-05
ROPE_BASE = 500000.0
CHUNK_EIGHTHS = (1, 1, 1, 1, 1, 1, 1, 1)


def shifted(block, axis, distance):
    devices = range(lax.axis_size(axis))
    route = [(i - distance, i) for i in devices if i - distance in devices]
    return lax.ppermute(block, axis, route)


def scatter_sum(blocks, axis):
    size = lax.axis_size(axis)
    current = blocks
    bit = 1
    while bit < size:
        half = current.shape[0] // 2
        keep, send = current[:half], current[half:]
        if bit >= 2:
            send = send.astype(jnp.bfloat16)
        pairs = [(i, i ^ bit) for i in range(size)]
        current = keep + lax.ppermute(send, axis, pairs).astype(jnp.float32)
        bit *= 2
    return current[0]


def all_sum(value, axis):
    size = lax.axis_size(axis)
    bit = 1
    while bit < size:
        value = value + lax.ppermute(value, axis, [(i, i ^ bit) for i in range(size)])
        bit *= 2
    return value


def bit_reversed(index, levels):
    return int(format(index, "0%db" % levels)[::-1], 2) if levels else 0


def rotate_keys(kv_cols, positions):
    head_size = kv_cols.shape[2]
    half_size = head_size // 2
    inverse = ROPE_BASE ** (-(jnp.arange(half_size, dtype=jnp.float32) * 2.0 / head_size))
    angles = inverse[:, None] * positions.astype(jnp.float32)[None, :]
    cosines = jnp.cos(angles)[None]
    sines = jnp.sin(angles)[None]
    key_part = kv_cols[:, 0]
    front_half = key_part[:, :half_size]
    back_half = key_part[:, half_size:]
    rotated = jnp.concatenate(
        [front_half * cosines - back_half * sines, back_half * cosines + front_half * sines],
        axis=1,
    )
    return jnp.stack([rotated, kv_cols[:, 1]], axis=1)


def per_device(hidden, owner, start, live, norm_gain, w_kv):
    groups = lax.axis_size("dp")
    tok_count = hidden.shape[2]
    capacity = 3 * tok_count // (2 * groups)
    slot_count = capacity * groups

    tok_rows = hidden[0, 0]
    target = owner[0, 0, :, 0]
    row_index = jnp.arange(tok_count, dtype=jnp.int32)
    row_alive = row_index < live[0, 0]
    onehot = (
        (target[:, None] == jnp.arange(groups, dtype=jnp.int32)[None, :]) & row_alive[:, None]
    ).astype(jnp.int32)
    row_rank = jnp.sum((jnp.cumsum(onehot, axis=0) - onehot) * onehot, axis=1)
    row_slot = jnp.where(row_alive, target * capacity + row_rank, slot_count)
    position = start[0, 0] + row_index
    widened = tok_rows.astype(jnp.float32)
    part_sq = jnp.sum(widened * widened, axis=1)
    meta = jnp.stack([part_sq, row_slot.astype(jnp.float32), position.astype(jnp.float32)])
    meta = shifted(meta, "section", 1)
    sum_sq = all_sum(meta[0], "tensor")

    first = lax.axis_index("section") == 0
    row_slot = jnp.where(first, slot_count, meta[1].astype(jnp.int32))
    position = meta[2].astype(jnp.int32)
    scale = lax.rsqrt(sum_sq / D + EPSILON)
    gain = norm_gain[0]
    weight = w_kv[0]
    local_width = tok_rows.shape[1]
    bounds = [local_width * sum(CHUNK_EIGHTHS[:k]) // 8 for k in range(len(CHUNK_EIGHTHS) + 1)]
    tensor = lax.axis_size("tensor")
    me_t = lax.axis_index("tensor")
    levels = tensor.bit_length() - 1
    block = weight.shape[1] // tensor
    partial = None
    for k in range(len(CHUNK_EIGHTHS)):
        cols = slice(bounds[k], bounds[k + 1])
        arrived = shifted(tok_rows[:, cols], "section", 1)
        normed = (arrived.astype(jnp.float32) * gain[cols] * scale[:, None]).astype(jnp.bfloat16)
        terms = []
        for s in range(tensor):
            column = jnp.bitwise_xor(me_t, bit_reversed(s, levels)) * block
            piece = lax.dynamic_slice_in_dim(weight[cols], column, block, axis=1)
            terms.append(
                lax.dot_general(
                    piece, normed, (((0,), (1,)), ((), ())), preferred_element_type=jnp.float32
                )
            )
        term = jnp.stack(terms)
        partial = term if partial is None else partial + term
    summed = scatter_sum(partial, "tensor")
    local_cols = summed.shape[0]
    local_kv = summed.reshape(local_cols // (2 * HD), 2, HD, tok_count)
    result = rotate_keys(local_kv, position).reshape(local_cols, tok_count).astype(jnp.bfloat16)

    placing = row_slot[None, :] == jnp.arange(slot_count, dtype=jnp.int32)[:, None]
    packed = lax.dot_general(
        placing.astype(jnp.bfloat16), result, (((1,), (1,)), ((), ())),
        preferred_element_type=jnp.float32,
    ).astype(jnp.bfloat16)
    packed = packed.reshape(groups, capacity, local_cols)
    me = lax.axis_index("dp")
    received = [None] * groups
    received[0] = lax.dynamic_index_in_dim(packed, me, 0, keepdims=False)
    for offset in range(1, groups):
        outgoing = lax.dynamic_index_in_dim(packed, (me + offset) % groups, 0, keepdims=False)
        pairs = [(i, (i + offset) % groups) for i in range(groups)]
        received[offset] = lax.ppermute(outgoing, "dp", pairs)
    stacked = jnp.stack(received)
    routed = jnp.take(stacked, (me - jnp.arange(groups, dtype=jnp.int32)) % groups, axis=0)
    return routed.reshape(1, 1, slot_count, local_cols)


def solution(mesh):
    in_specs = (
        P("section", "dp", None, "tensor"),
        P("section", "dp", None, None),
        P("section", "dp"),
        P("section", "dp"),
        P("section", "tensor"),
        P("section", "tensor", None),
    )
    out_specs = P("section", "dp", None, "tensor")
    return jax.shard_map(
        per_device, mesh=mesh, in_specs=in_specs, out_specs=out_specs, check_vma=False
    )
```

```python
import jax
import jax.numpy as jnp
from jax import lax
from jax.sharding import PartitionSpec as P

D = 16384
HD = 128


EPSILON = 1e-05
ROPE_BASE = 500000.0
CHUNK_EIGHTHS = (1, 1, 1, 1, 1, 1, 1, 1)


def shifted(block, axis, distance):
    devices = range(lax.axis_size(axis))
    route = [(i - distance, i) for i in devices if i - distance in devices]
    return lax.ppermute(block, axis, route)


def scatter_sum(blocks, axis):
    size = lax.axis_size(axis)
    current = blocks
    bit = 1
    while bit < size:
        half = current.shape[0] // 2
        keep, send = current[:half], current[half:]
        if bit >= 2:
            send = send.astype(jnp.bfloat16)
        pairs = [(i, i ^ bit) for i in range(size)]
        current = keep + lax.ppermute(send, axis, pairs).astype(jnp.float32)
        bit *= 2
    return current[0]


def all_sum(value, axis):
    size = lax.axis_size(axis)
    bit = 1
    while bit < size:
        value = value + lax.ppermute(value, axis, [(i, i ^ bit) for i in range(size)])
        bit *= 2
    return value


def bit_reversed(index, levels):
    return int(format(index, "0%db" % levels)[::-1], 2) if levels else 0


def rotate_keys(kv_cols, positions):
    head_size = kv_cols.shape[2]
    half_size = head_size // 2
    inverse = ROPE_BASE ** (-(jnp.arange(half_size, dtype=jnp.float32) * 2.0 / head_size))
    angles = inverse[:, None] * positions.astype(jnp.float32)[None, :]
    cosines = jnp.cos(angles)[None]
    sines = jnp.sin(angles)[None]
    key_part = kv_cols[:, 0]
    front_half = key_part[:, :half_size]
    back_half = key_part[:, half_size:]
    rotated = jnp.concatenate(
        [front_half * cosines - back_half * sines, back_half * cosines + front_half * sines],
        axis=1,
    )
    return jnp.stack([rotated, kv_cols[:, 1]], axis=1)


def per_device(hidden, owner, start, live, norm_gain, w_kv):
    groups = lax.axis_size("dp")
    tok_count = hidden.shape[2]
    capacity = 3 * tok_count // (2 * groups)
    slot_count = capacity * groups

    tok_rows = hidden[0, 0]
    target = owner[0, 0, :, 0]
    row_index = jnp.arange(tok_count, dtype=jnp.int32)
    row_alive = row_index < live[0, 0]
    onehot = (
        (target[:, None] == jnp.arange(groups, dtype=jnp.int32)[None, :]) & row_alive[:, None]
    ).astype(jnp.int32)
    row_rank = jnp.sum((jnp.cumsum(onehot, axis=0) - onehot) * onehot, axis=1)
    row_slot = jnp.where(row_alive, target * capacity + row_rank, slot_count)
    position = start[0, 0] + row_index
    widened = tok_rows.astype(jnp.float32)
    part_sq = jnp.sum(widened * widened, axis=1)
    meta = jnp.stack([part_sq, row_slot.astype(jnp.float32), position.astype(jnp.float32)])
    meta = shifted(meta, "section", 1)
    sum_sq = all_sum(meta[0], "tensor")

    first = lax.axis_index("section") == 0
    row_slot = jnp.where(first, slot_count, meta[1].astype(jnp.int32))
    position = meta[2].astype(jnp.int32)
    scale = lax.rsqrt(sum_sq / D + EPSILON)
    gain = norm_gain[0]
    weight = w_kv[0]
    local_width = tok_rows.shape[1]
    bounds = [local_width * sum(CHUNK_EIGHTHS[:k]) // 8 for k in range(len(CHUNK_EIGHTHS) + 1)]
    tensor = lax.axis_size("tensor")
    me_t = lax.axis_index("tensor")
    levels = tensor.bit_length() - 1
    block = weight.shape[1] // tensor
    partial = None
    for k in range(len(CHUNK_EIGHTHS)):
        cols = slice(bounds[k], bounds[k + 1])
        arrived = shifted(tok_rows[:, cols], "section", 1)
        normed = (arrived.astype(jnp.float32) * gain[cols] * scale[:, None]).astype(jnp.bfloat16)
        term = jnp.stack([
            lax.dot_general(
                weight[cols, j * block:(j + 1) * block], normed, (((0,), (1,)), ((), ())),
                preferred_element_type=jnp.float32,
            )
            for j in range(tensor)
        ])
        partial = term if partial is None else partial + term
    order = jnp.bitwise_xor(
        me_t, jnp.array([bit_reversed(s, levels) for s in range(tensor)], dtype=jnp.int32)
    )
    partial = jnp.take(partial, order, axis=0)
    summed = scatter_sum(partial, "tensor")
    local_cols = summed.shape[0]
    local_kv = summed.reshape(local_cols // (2 * HD), 2, HD, tok_count)
    result = rotate_keys(local_kv, position).reshape(local_cols, tok_count).astype(jnp.bfloat16)

    placing = row_slot[None, :] == jnp.arange(slot_count, dtype=jnp.int32)[:, None]
    packed = lax.dot_general(
        placing.astype(jnp.bfloat16), result, (((1,), (1,)), ((), ())),
        preferred_element_type=jnp.float32,
    ).astype(jnp.bfloat16)
    packed = packed.reshape(groups, capacity, local_cols)
    me = lax.axis_index("dp")
    received = [None] * groups
    received[0] = lax.dynamic_index_in_dim(packed, me, 0, keepdims=False)
    for offset in range(1, groups):
        outgoing = lax.dynamic_index_in_dim(packed, (me + offset) % groups, 0, keepdims=False)
        pairs = [(i, (i + offset) % groups) for i in range(groups)]
        received[offset] = lax.ppermute(outgoing, "dp", pairs)
    stacked = jnp.stack(received)
    routed = jnp.take(stacked, (me - jnp.arange(groups, dtype=jnp.int32)) % groups, axis=0)
    return routed.reshape(1, 1, slot_count, local_cols)


def solution(mesh):
    in_specs = (
        P("section", "dp", None, "tensor"),
        P("section", "dp", None, None),
        P("section", "dp"),
        P("section", "dp"),
        P("section", "tensor"),
        P("section", "tensor", None),
    )
    out_specs = P("section", "dp", None, "tensor")
    return jax.shard_map(
        per_device, mesh=mesh, in_specs=in_specs, out_specs=out_specs, check_vma=False
    )
```

```python
import jax
import jax.numpy as jnp
from jax import lax
from jax.sharding import PartitionSpec as P

D = 16384
HD = 128


EPSILON = 1e-05
ROPE_BASE = 500000.0
CHUNK_EIGHTHS = (2, 2, 2, 1, 1)


def shifted(block, axis, distance):
    devices = range(lax.axis_size(axis))
    route = [(i - distance, i) for i in devices if i - distance in devices]
    return lax.ppermute(block, axis, route)


def scatter_sum(blocks, axis):
    size = lax.axis_size(axis)
    current = blocks
    bit = 1
    while bit < size:
        half = current.shape[0] // 2
        keep, send = current[:half], current[half:]
        if bit >= 2:
            send = send.astype(jnp.bfloat16)
        pairs = [(i, i ^ bit) for i in range(size)]
        current = keep + lax.ppermute(send, axis, pairs).astype(jnp.float32)
        bit *= 2
    return current[0]


def all_sum(value, axis):
    size = lax.axis_size(axis)
    bit = 1
    while bit < size:
        value = value + lax.ppermute(value, axis, [(i, i ^ bit) for i in range(size)])
        bit *= 2
    return value


def bit_reversed(index, levels):
    return int(format(index, "0%db" % levels)[::-1], 2) if levels else 0


def rotate_keys(kv_cols, positions):
    head_size = kv_cols.shape[2]
    half_size = head_size // 2
    inverse = ROPE_BASE ** (-(jnp.arange(half_size, dtype=jnp.float32) * 2.0 / head_size))
    angles = inverse[:, None] * positions.astype(jnp.float32)[None, :]
    cosines = jnp.cos(angles)[None]
    sines = jnp.sin(angles)[None]
    key_part = kv_cols[:, 0]
    front_half = key_part[:, :half_size]
    back_half = key_part[:, half_size:]
    rotated = jnp.concatenate(
        [front_half * cosines - back_half * sines, back_half * cosines + front_half * sines],
        axis=1,
    )
    return jnp.stack([rotated, kv_cols[:, 1]], axis=1)


def per_device(hidden, owner, start, live, norm_gain, w_kv):
    groups = lax.axis_size("dp")
    tok_count = hidden.shape[2]
    capacity = 3 * tok_count // (2 * groups)
    slot_count = capacity * groups

    tok_rows = hidden[0, 0]
    target = owner[0, 0, :, 0]
    row_index = jnp.arange(tok_count, dtype=jnp.int32)
    row_alive = row_index < live[0, 0]
    onehot = (
        (target[:, None] == jnp.arange(groups, dtype=jnp.int32)[None, :]) & row_alive[:, None]
    ).astype(jnp.int32)
    row_rank = jnp.sum((jnp.cumsum(onehot, axis=0) - onehot) * onehot, axis=1)
    row_slot = jnp.where(row_alive, target * capacity + row_rank, slot_count)
    position = start[0, 0] + row_index
    widened = tok_rows.astype(jnp.float32)
    part_sq = jnp.sum(widened * widened, axis=1)
    meta = jnp.stack([part_sq, row_slot.astype(jnp.float32), position.astype(jnp.float32)])
    meta = shifted(meta, "section", 1)
    sum_sq = all_sum(meta[0], "tensor")

    first = lax.axis_index("section") == 0
    row_slot = jnp.where(first, slot_count, meta[1].astype(jnp.int32))
    position = meta[2].astype(jnp.int32)
    scale = lax.rsqrt(sum_sq / D + EPSILON)
    gain = norm_gain[0]
    weight = w_kv[0]
    local_width = tok_rows.shape[1]
    bounds = [local_width * sum(CHUNK_EIGHTHS[:k]) // 8 for k in range(len(CHUNK_EIGHTHS) + 1)]
    tensor = lax.axis_size("tensor")
    me_t = lax.axis_index("tensor")
    levels = tensor.bit_length() - 1
    block = weight.shape[1] // tensor
    partial = None
    for k in range(len(CHUNK_EIGHTHS)):
        cols = slice(bounds[k], bounds[k + 1])
        arrived = shifted(tok_rows[:, cols], "section", 1)
        if partial is not None:
            partial, arrived = lax.optimization_barrier((partial, arrived))
        normed = (arrived.astype(jnp.float32) * gain[cols] * scale[:, None]).astype(jnp.bfloat16)
        terms = []
        for s in range(tensor):
            column = jnp.bitwise_xor(me_t, bit_reversed(s, levels)) * block
            piece = lax.dynamic_slice_in_dim(weight[cols], column, block, axis=1)
            terms.append(
                lax.dot_general(
                    piece, normed, (((0,), (1,)), ((), ())), preferred_element_type=jnp.float32
                )
            )
        term = jnp.stack(terms)
        partial = term if partial is None else partial + term
    summed = scatter_sum(partial, "tensor")
    local_cols = summed.shape[0]
    local_kv = summed.reshape(local_cols // (2 * HD), 2, HD, tok_count)
    result = rotate_keys(local_kv, position).reshape(local_cols, tok_count).astype(jnp.bfloat16)

    placing = row_slot[None, :] == jnp.arange(slot_count, dtype=jnp.int32)[:, None]
    packed = lax.dot_general(
        placing.astype(jnp.bfloat16), result, (((1,), (1,)), ((), ())),
        preferred_element_type=jnp.float32,
    ).astype(jnp.bfloat16)
    packed = packed.reshape(groups, capacity, local_cols)
    me = lax.axis_index("dp")
    received = [None] * groups
    received[0] = lax.dynamic_index_in_dim(packed, me, 0, keepdims=False)
    for offset in range(1, groups):
        outgoing = lax.dynamic_index_in_dim(packed, (me + offset) % groups, 0, keepdims=False)
        pairs = [(i, (i + offset) % groups) for i in range(groups)]
        received[offset] = lax.ppermute(outgoing, "dp", pairs)
    stacked = jnp.stack(received)
    routed = jnp.take(stacked, (me - jnp.arange(groups, dtype=jnp.int32)) % groups, axis=0)
    return routed.reshape(1, 1, slot_count, local_cols)


def solution(mesh):
    in_specs = (
        P("section", "dp", None, "tensor"),
        P("section", "dp", None, None),
        P("section", "dp"),
        P("section", "dp"),
        P("section", "tensor"),
        P("section", "tensor", None),
    )
    out_specs = P("section", "dp", None, "tensor")
    return jax.shard_map(
        per_device, mesh=mesh, in_specs=in_specs, out_specs=out_specs, check_vma=False
    )
```

```python
import jax
import jax.numpy as jnp
from jax import lax
from jax.sharding import PartitionSpec as P

D = 16384
HD = 128


EPSILON = 1e-05
ROPE_BASE = 500000.0
CHUNK_EIGHTHS = (2, 2, 2, 2)


def shifted(block, axis, distance):
    devices = range(lax.axis_size(axis))
    route = [(i - distance, i) for i in devices if i - distance in devices]
    return lax.ppermute(block, axis, route)


def scatter_sum(blocks, axis):
    size = lax.axis_size(axis)
    current = blocks
    bit = 1
    while bit < size:
        half = current.shape[0] // 2
        keep, send = current[:half], current[half:]
        if bit >= 2:
            send = send.astype(jnp.bfloat16)
        pairs = [(i, i ^ bit) for i in range(size)]
        current = keep + lax.ppermute(send, axis, pairs).astype(jnp.float32)
        bit *= 2
    return current[0]


def all_sum(value, axis):
    size = lax.axis_size(axis)
    bit = 1
    while bit < size:
        value = value + lax.ppermute(value, axis, [(i, i ^ bit) for i in range(size)])
        bit *= 2
    return value


def bit_reversed(index, levels):
    return int(format(index, "0%db" % levels)[::-1], 2) if levels else 0


def rotate_keys(kv_cols, positions):
    head_size = kv_cols.shape[2]
    half_size = head_size // 2
    inverse = ROPE_BASE ** (-(jnp.arange(half_size, dtype=jnp.float32) * 2.0 / head_size))
    angles = inverse[:, None] * positions.astype(jnp.float32)[None, :]
    cosines = jnp.cos(angles)[None]
    sines = jnp.sin(angles)[None]
    key_part = kv_cols[:, 0]
    front_half = key_part[:, :half_size]
    back_half = key_part[:, half_size:]
    rotated = jnp.concatenate(
        [front_half * cosines - back_half * sines, back_half * cosines + front_half * sines],
        axis=1,
    )
    return jnp.stack([rotated, kv_cols[:, 1]], axis=1)


def per_device(hidden, owner, start, live, norm_gain, w_kv):
    groups = lax.axis_size("dp")
    tok_count = hidden.shape[2]
    capacity = 3 * tok_count // (2 * groups)
    slot_count = capacity * groups

    tok_rows = hidden[0, 0]
    target = owner[0, 0, :, 0]
    row_index = jnp.arange(tok_count, dtype=jnp.int32)
    row_alive = row_index < live[0, 0]
    onehot = (
        (target[:, None] == jnp.arange(groups, dtype=jnp.int32)[None, :]) & row_alive[:, None]
    ).astype(jnp.int32)
    row_rank = jnp.sum((jnp.cumsum(onehot, axis=0) - onehot) * onehot, axis=1)
    row_slot = jnp.where(row_alive, target * capacity + row_rank, slot_count)
    position = start[0, 0] + row_index
    widened = tok_rows.astype(jnp.float32)
    part_sq = jnp.sum(widened * widened, axis=1)
    meta = jnp.stack([part_sq, row_slot.astype(jnp.float32), position.astype(jnp.float32)])
    meta = shifted(meta, "section", 1)
    sum_sq = all_sum(meta[0], "tensor")

    first = lax.axis_index("section") == 0
    row_slot = jnp.where(first, slot_count, meta[1].astype(jnp.int32))
    position = meta[2].astype(jnp.int32)
    scale = lax.rsqrt(sum_sq / D + EPSILON)
    gain = norm_gain[0]
    weight = w_kv[0]
    local_width = tok_rows.shape[1]
    bounds = [local_width * sum(CHUNK_EIGHTHS[:k]) // 8 for k in range(len(CHUNK_EIGHTHS) + 1)]
    tensor = lax.axis_size("tensor")
    me_t = lax.axis_index("tensor")
    levels = tensor.bit_length() - 1
    block = weight.shape[1] // tensor
    partial = None
    for k in range(len(CHUNK_EIGHTHS)):
        cols = slice(bounds[k], bounds[k + 1])
        arrived = shifted(tok_rows[:, cols], "section", 1)
        normed = (arrived.astype(jnp.float32) * gain[cols] * scale[:, None]).astype(jnp.bfloat16)
        terms = []
        for s in range(tensor):
            column = jnp.bitwise_xor(me_t, bit_reversed(s, levels)) * block
            piece = lax.dynamic_slice_in_dim(weight[cols], column, block, axis=1)
            terms.append(
                lax.dot_general(
                    piece, normed, (((0,), (1,)), ((), ())), preferred_element_type=jnp.float32
                )
            )
        term = jnp.stack(terms)
        partial = term if partial is None else partial + term
    summed = scatter_sum(partial, "tensor")
    local_cols = summed.shape[0]
    local_kv = summed.reshape(local_cols // (2 * HD), 2, HD, tok_count)
    result = rotate_keys(local_kv, position).reshape(local_cols, tok_count).astype(jnp.bfloat16)

    placing = row_slot[None, :] == jnp.arange(slot_count, dtype=jnp.int32)[:, None]
    packed = lax.dot_general(
        placing.astype(jnp.bfloat16), result, (((1,), (1,)), ((), ())),
        preferred_element_type=jnp.float32,
    ).astype(jnp.bfloat16)
    packed = packed.reshape(groups, capacity, local_cols)
    me = lax.axis_index("dp")
    received = [None] * groups
    received[0] = lax.dynamic_index_in_dim(packed, me, 0, keepdims=False)
    for offset in range(1, groups):
        outgoing = lax.dynamic_index_in_dim(packed, (me + offset) % groups, 0, keepdims=False)
        pairs = [(i, (i + offset) % groups) for i in range(groups)]
        received[offset] = lax.ppermute(outgoing, "dp", pairs)
    stacked = jnp.stack(received)
    routed = jnp.take(stacked, (me - jnp.arange(groups, dtype=jnp.int32)) % groups, axis=0)
    return routed.reshape(1, 1, slot_count, local_cols)


def solution(mesh):
    in_specs = (
        P("section", "dp", None, "tensor"),
        P("section", "dp", None, None),
        P("section", "dp"),
        P("section", "dp"),
        P("section", "tensor"),
        P("section", "tensor", None),
    )
    out_specs = P("section", "dp", None, "tensor")
    return jax.shard_map(
        per_device, mesh=mesh, in_specs=in_specs, out_specs=out_specs, check_vma=False
    )
```

```python
import jax
import jax.numpy as jnp
from jax import lax
from jax.sharding import PartitionSpec as P

D = 16384
HD = 128


EPSILON = 1e-05
ROPE_BASE = 500000.0
CHUNK_EIGHTHS = (2, 2, 2, 2)


def shifted(block, axis, distance):
    devices = range(lax.axis_size(axis))
    route = [(i - distance, i) for i in devices if i - distance in devices]
    return lax.ppermute(block, axis, route)


def scatter_sum(blocks, axis):
    size = lax.axis_size(axis)
    current = blocks
    bit = 1
    while bit < size:
        half = current.shape[0] // 2
        keep, send = current[:half], current[half:]
        if bit >= 2:
            send = send.astype(jnp.bfloat16)
        pairs = [(i, i ^ bit) for i in range(size)]
        current = keep + lax.ppermute(send, axis, pairs).astype(jnp.float32)
        bit *= 2
    return current[0]


def all_sum(value, axis):
    size = lax.axis_size(axis)
    bit = 1
    while bit < size:
        value = value + lax.ppermute(value, axis, [(i, i ^ bit) for i in range(size)])
        bit *= 2
    return value


def bit_reversed(index, levels):
    return int(format(index, "0%db" % levels)[::-1], 2) if levels else 0


def rotate_keys(kv_cols, positions):
    head_size = kv_cols.shape[2]
    half_size = head_size // 2
    inverse = ROPE_BASE ** (-(jnp.arange(half_size, dtype=jnp.float32) * 2.0 / head_size))
    angles = inverse[:, None] * positions.astype(jnp.float32)[None, :]
    cosines = jnp.cos(angles)[None]
    sines = jnp.sin(angles)[None]
    key_part = kv_cols[:, 0]
    front_half = key_part[:, :half_size]
    back_half = key_part[:, half_size:]
    rotated = jnp.concatenate(
        [front_half * cosines - back_half * sines, back_half * cosines + front_half * sines],
        axis=1,
    )
    return jnp.stack([rotated, kv_cols[:, 1]], axis=1)


def per_device(hidden, owner, start, live, norm_gain, w_kv):
    groups = lax.axis_size("dp")
    tok_count = hidden.shape[2]
    capacity = 3 * tok_count // (2 * groups)
    slot_count = capacity * groups

    tok_rows = hidden[0, 0]
    target = owner[0, 0, :, 0]
    row_index = jnp.arange(tok_count, dtype=jnp.int32)
    row_alive = row_index < live[0, 0]
    onehot = (
        (target[:, None] == jnp.arange(groups, dtype=jnp.int32)[None, :]) & row_alive[:, None]
    ).astype(jnp.int32)
    row_rank = jnp.sum((jnp.cumsum(onehot, axis=0) - onehot) * onehot, axis=1)
    row_slot = jnp.where(row_alive, target * capacity + row_rank, slot_count)
    position = start[0, 0] + row_index
    widened = tok_rows.astype(jnp.float32)
    part_sq = jnp.sum(widened * widened, axis=1)
    meta = jnp.stack([part_sq, row_slot.astype(jnp.float32), position.astype(jnp.float32)])
    meta = shifted(meta, "section", 1)
    sum_sq = all_sum(meta[0], "tensor")

    first = lax.axis_index("section") == 0
    row_slot = jnp.where(first, slot_count, meta[1].astype(jnp.int32))
    position = meta[2].astype(jnp.int32)
    scale = lax.rsqrt(sum_sq / D + EPSILON)
    gain = norm_gain[0]
    weight = w_kv[0]
    local_width = tok_rows.shape[1]
    bounds = [local_width * sum(CHUNK_EIGHTHS[:k]) // 8 for k in range(len(CHUNK_EIGHTHS) + 1)]
    tensor = lax.axis_size("tensor")
    me_t = lax.axis_index("tensor")
    levels = tensor.bit_length() - 1
    block = weight.shape[1] // tensor
    partial = None
    for k in range(len(CHUNK_EIGHTHS)):
        cols = slice(bounds[k], bounds[k + 1])
        arrived = shifted(tok_rows[:, cols], "section", 1)
        def project(arrived=arrived, cols=cols):
            normed = (arrived.astype(jnp.float32) * gain[cols] * scale[:, None]).astype(jnp.bfloat16)
            terms = []
            for s in range(tensor):
                column = jnp.bitwise_xor(me_t, bit_reversed(s, levels)) * block
                piece = lax.dynamic_slice_in_dim(weight[cols], column, block, axis=1)
                terms.append(
                    lax.dot_general(
                        piece, normed, (((0,), (1,)), ((), ())), preferred_element_type=jnp.float32
                    )
                )
            return jnp.stack(terms)

        term = lax.cond(
            first,
            lambda: jnp.zeros((tensor, block, tok_count), jnp.float32),
            project,
        )
        partial = term if partial is None else partial + term
    summed = scatter_sum(partial, "tensor")
    local_cols = summed.shape[0]
    local_kv = summed.reshape(local_cols // (2 * HD), 2, HD, tok_count)
    result = rotate_keys(local_kv, position).reshape(local_cols, tok_count).astype(jnp.bfloat16)

    placing = row_slot[None, :] == jnp.arange(slot_count, dtype=jnp.int32)[:, None]
    packed = lax.dot_general(
        placing.astype(jnp.bfloat16), result, (((1,), (1,)), ((), ())),
        preferred_element_type=jnp.float32,
    ).astype(jnp.bfloat16)
    packed = packed.reshape(groups, capacity, local_cols)
    me = lax.axis_index("dp")
    received = [None] * groups
    received[0] = lax.dynamic_index_in_dim(packed, me, 0, keepdims=False)
    for offset in range(1, groups):
        outgoing = lax.dynamic_index_in_dim(packed, (me + offset) % groups, 0, keepdims=False)
        pairs = [(i, (i + offset) % groups) for i in range(groups)]
        received[offset] = lax.ppermute(outgoing, "dp", pairs)
    stacked = jnp.stack(received)
    routed = jnp.take(stacked, (me - jnp.arange(groups, dtype=jnp.int32)) % groups, axis=0)
    return routed.reshape(1, 1, slot_count, local_cols)


def solution(mesh):
    in_specs = (
        P("section", "dp", None, "tensor"),
        P("section", "dp", None, None),
        P("section", "dp"),
        P("section", "dp"),
        P("section", "tensor"),
        P("section", "tensor", None),
    )
    out_specs = P("section", "dp", None, "tensor")
    return jax.shard_map(
        per_device, mesh=mesh, in_specs=in_specs, out_specs=out_specs, check_vma=False
    )
```

```python
import jax
import jax.numpy as jnp
from jax import lax
from jax.sharding import PartitionSpec as P

D = 16384
HD = 128


EPSILON = 1e-05
ROPE_BASE = 500000.0
CHUNK_EIGHTHS = (2, 2, 2, 2)


def shifted(block, axis, distance):
    devices = range(lax.axis_size(axis))
    route = [(i - distance, i) for i in devices if i - distance in devices]
    return lax.ppermute(block, axis, route)


def scatter_sum(blocks, axis):
    size = lax.axis_size(axis)
    current = blocks
    bit = 1
    while bit < size:
        half = current.shape[0] // 2
        keep, send = current[:half], current[half:]
        if bit >= 2:
            send = send.astype(jnp.bfloat16)
        pairs = [(i, i ^ bit) for i in range(size)]
        current = keep + lax.ppermute(send, axis, pairs).astype(jnp.float32)
        bit *= 2
    return current[0]


def all_sum(value, axis):
    size = lax.axis_size(axis)
    bit = 1
    while bit < size:
        value = value + lax.ppermute(value, axis, [(i, i ^ bit) for i in range(size)])
        bit *= 2
    return value


def bit_reversed(index, levels):
    return int(format(index, "0%db" % levels)[::-1], 2) if levels else 0


def rotate_keys(kv_cols, positions):
    head_size = kv_cols.shape[2]
    half_size = head_size // 2
    inverse = ROPE_BASE ** (-(jnp.arange(half_size, dtype=jnp.float32) * 2.0 / head_size))
    angles = inverse[:, None] * positions.astype(jnp.float32)[None, :]
    cosines = jnp.cos(angles)[None]
    sines = jnp.sin(angles)[None]
    key_part = kv_cols[:, 0]
    front_half = key_part[:, :half_size]
    back_half = key_part[:, half_size:]
    rotated = jnp.concatenate(
        [front_half * cosines - back_half * sines, back_half * cosines + front_half * sines],
        axis=1,
    )
    return jnp.stack([rotated, kv_cols[:, 1]], axis=1)


def per_device(hidden, owner, start, live, norm_gain, w_kv):
    groups = lax.axis_size("dp")
    tok_count = hidden.shape[2]
    capacity = 3 * tok_count // (2 * groups)
    slot_count = capacity * groups

    tok_rows = hidden[0, 0]
    target = owner[0, 0, :, 0]
    row_index = jnp.arange(tok_count, dtype=jnp.int32)
    row_alive = row_index < live[0, 0]
    onehot = (
        (target[:, None] == jnp.arange(groups, dtype=jnp.int32)[None, :]) & row_alive[:, None]
    ).astype(jnp.int32)
    row_rank = jnp.sum((jnp.cumsum(onehot, axis=0) - onehot) * onehot, axis=1)
    row_slot = jnp.where(row_alive, target * capacity + row_rank, slot_count)
    position = start[0, 0] + row_index
    widened = tok_rows.astype(jnp.float32)
    part_sq = jnp.sum(widened * widened, axis=1)
    meta = jnp.stack([part_sq, row_slot.astype(jnp.float32), position.astype(jnp.float32)])
    meta = shifted(meta, "section", 1)
    sum_sq = all_sum(meta[0], "tensor")

    first = lax.axis_index("section") == 0
    row_slot = jnp.where(first, slot_count, meta[1].astype(jnp.int32))
    position = meta[2].astype(jnp.int32)
    scale = lax.rsqrt(sum_sq / D + EPSILON)
    gain = norm_gain[0]
    weight = w_kv[0]
    local_width = tok_rows.shape[1]
    bounds = [local_width * sum(CHUNK_EIGHTHS[:k]) // 8 for k in range(len(CHUNK_EIGHTHS) + 1)]
    tensor = lax.axis_size("tensor")
    me_t = lax.axis_index("tensor")
    levels = tensor.bit_length() - 1
    block = weight.shape[1] // tensor
    partial = None
    for k in range(len(CHUNK_EIGHTHS)):
        cols = slice(bounds[k], bounds[k + 1])
        arrived = shifted(tok_rows[:, cols], "section", 1)
        if partial is not None:
            partial, arrived = lax.optimization_barrier((partial, arrived))
        normed = (arrived.astype(jnp.float32) * gain[cols] * scale[:, None]).astype(jnp.bfloat16)
        for low in range(bounds[k], bounds[k + 1], local_width // 8):
            part = slice(low, low + local_width // 8)
            sub = normed[:, low - bounds[k]:low - bounds[k] + local_width // 8]
            terms = []
            for s in range(tensor):
                column = jnp.bitwise_xor(me_t, bit_reversed(s, levels)) * block
                piece = lax.dynamic_slice_in_dim(weight[part], column, block, axis=1)
                terms.append(
                    lax.dot_general(
                        piece, sub, (((0,), (1,)), ((), ())), preferred_element_type=jnp.float32
                    )
                )
            term = jnp.stack(terms)
            partial = term if partial is None else partial + term
    summed = scatter_sum(partial, "tensor")
    local_cols = summed.shape[0]
    local_kv = summed.reshape(local_cols // (2 * HD), 2, HD, tok_count)
    result = rotate_keys(local_kv, position).reshape(local_cols, tok_count).astype(jnp.bfloat16)

    placing = row_slot[None, :] == jnp.arange(slot_count, dtype=jnp.int32)[:, None]
    packed = lax.dot_general(
        placing.astype(jnp.bfloat16), result, (((1,), (1,)), ((), ())),
        preferred_element_type=jnp.float32,
    ).astype(jnp.bfloat16)
    packed = packed.reshape(groups, capacity, local_cols)
    me = lax.axis_index("dp")
    received = [None] * groups
    received[0] = lax.dynamic_index_in_dim(packed, me, 0, keepdims=False)
    for offset in range(1, groups):
        outgoing = lax.dynamic_index_in_dim(packed, (me + offset) % groups, 0, keepdims=False)
        pairs = [(i, (i + offset) % groups) for i in range(groups)]
        received[offset] = lax.ppermute(outgoing, "dp", pairs)
    stacked = jnp.stack(received)
    routed = jnp.take(stacked, (me - jnp.arange(groups, dtype=jnp.int32)) % groups, axis=0)
    return routed.reshape(1, 1, slot_count, local_cols)


def solution(mesh):
    in_specs = (
        P("section", "dp", None, "tensor"),
        P("section", "dp", None, None),
        P("section", "dp"),
        P("section", "dp"),
        P("section", "tensor"),
        P("section", "tensor", None),
    )
    out_specs = P("section", "dp", None, "tensor")
    return jax.shard_map(
        per_device, mesh=mesh, in_specs=in_specs, out_specs=out_specs, check_vma=False
    )
```

```python
import jax
import jax.numpy as jnp
from jax import lax
from jax.sharding import PartitionSpec as P

D = 16384
HD = 128


EPSILON = 1e-05
ROPE_BASE = 500000.0
CHUNK_EIGHTHS = (2, 2, 2, 2)


def shifted(block, axis, distance):
    devices = range(lax.axis_size(axis))
    route = [(i - distance, i) for i in devices if i - distance in devices]
    return lax.ppermute(block, axis, route)


def scatter_sum(blocks, axis):
    size = lax.axis_size(axis)
    current = blocks
    bit = 1
    while bit < size:
        half = current.shape[0] // 2
        keep, send = current[:half], current[half:]
        if bit >= 2:
            send = send.astype(jnp.bfloat16)
        pairs = [(i, i ^ bit) for i in range(size)]
        current = keep + lax.ppermute(send, axis, pairs).astype(jnp.float32)
        bit *= 2
    return current[0]


def all_sum(value, axis):
    size = lax.axis_size(axis)
    bit = 1
    while bit < size:
        value = value + lax.ppermute(value, axis, [(i, i ^ bit) for i in range(size)])
        bit *= 2
    return value


def bit_reversed(index, levels):
    return int(format(index, "0%db" % levels)[::-1], 2) if levels else 0


def rotate_keys(kv_cols, positions):
    head_size = kv_cols.shape[2]
    half_size = head_size // 2
    inverse = ROPE_BASE ** (-(jnp.arange(half_size, dtype=jnp.float32) * 2.0 / head_size))
    angles = inverse[:, None] * positions.astype(jnp.float32)[None, :]
    cosines = jnp.cos(angles)[None]
    sines = jnp.sin(angles)[None]
    key_part = kv_cols[:, 0]
    front_half = key_part[:, :half_size]
    back_half = key_part[:, half_size:]
    rotated = jnp.concatenate(
        [front_half * cosines - back_half * sines, back_half * cosines + front_half * sines],
        axis=1,
    )
    return jnp.stack([rotated, kv_cols[:, 1]], axis=1)


def per_device(hidden, owner, start, live, norm_gain, w_kv):
    groups = lax.axis_size("dp")
    tok_count = hidden.shape[2]
    capacity = 3 * tok_count // (2 * groups)
    slot_count = capacity * groups

    tok_rows = hidden[0, 0]
    target = owner[0, 0, :, 0]
    row_index = jnp.arange(tok_count, dtype=jnp.int32)
    row_alive = row_index < live[0, 0]
    onehot = (
        (target[:, None] == jnp.arange(groups, dtype=jnp.int32)[None, :]) & row_alive[:, None]
    ).astype(jnp.int32)
    row_rank = jnp.sum((jnp.cumsum(onehot, axis=0) - onehot) * onehot, axis=1)
    row_slot = jnp.where(row_alive, target * capacity + row_rank, slot_count)
    position = start[0, 0] + row_index
    widened = tok_rows.astype(jnp.float32)
    part_sq = jnp.sum(widened * widened, axis=1)
    meta = jnp.stack([part_sq, row_slot.astype(jnp.float32), position.astype(jnp.float32)])
    meta = shifted(meta, "section", 1)
    sum_sq = all_sum(meta[0], "tensor")

    first = lax.axis_index("section") == 0
    row_slot = jnp.where(first, slot_count, meta[1].astype(jnp.int32))
    position = meta[2].astype(jnp.int32)
    scale = lax.rsqrt(sum_sq / D + EPSILON)
    gain = norm_gain[0]
    weight = w_kv[0]
    local_width = tok_rows.shape[1]
    bounds = [local_width * sum(CHUNK_EIGHTHS[:k]) // 8 for k in range(len(CHUNK_EIGHTHS) + 1)]
    tensor = lax.axis_size("tensor")
    me_t = lax.axis_index("tensor")
    levels = tensor.bit_length() - 1
    block = weight.shape[1] // tensor
    partial = None
    for k in range(len(CHUNK_EIGHTHS)):
        cols = slice(bounds[k], bounds[k + 1])
        arrived = shifted(tok_rows[:, cols], "section", 1)
        if partial is not None:
            partial, arrived = lax.optimization_barrier((partial, arrived))
        normed = (arrived.astype(jnp.float32) * gain[cols] * scale[:, None]).astype(jnp.bfloat16)
        for low in range(bounds[k], bounds[k + 1], local_width // 8):
            part = slice(low, low + local_width // 8)
            sub = normed[:, low - bounds[k]:low - bounds[k] + local_width // 8]
            terms = []
            for s in range(tensor):
                column = jnp.bitwise_xor(me_t, bit_reversed(s, levels)) * block
                piece = lax.dynamic_slice(weight, (low, column), (local_width // 8, block))
                terms.append(
                    lax.dot_general(
                        piece, sub, (((0,), (1,)), ((), ())), preferred_element_type=jnp.float32
                    )
                )
            term = jnp.stack(terms)
            partial = term if partial is None else partial + term
    summed = scatter_sum(partial, "tensor")
    local_cols = summed.shape[0]
    local_kv = summed.reshape(local_cols // (2 * HD), 2, HD, tok_count)
    result = rotate_keys(local_kv, position).reshape(local_cols, tok_count).astype(jnp.bfloat16)

    placing = row_slot[None, :] == jnp.arange(slot_count, dtype=jnp.int32)[:, None]
    packed = lax.dot_general(
        placing.astype(jnp.bfloat16), result, (((1,), (1,)), ((), ())),
        preferred_element_type=jnp.float32,
    ).astype(jnp.bfloat16)
    packed = packed.reshape(groups, capacity, local_cols)
    me = lax.axis_index("dp")
    received = [None] * groups
    received[0] = lax.dynamic_index_in_dim(packed, me, 0, keepdims=False)
    for offset in range(1, groups):
        outgoing = lax.dynamic_index_in_dim(packed, (me + offset) % groups, 0, keepdims=False)
        pairs = [(i, (i + offset) % groups) for i in range(groups)]
        received[offset] = lax.ppermute(outgoing, "dp", pairs)
    stacked = jnp.stack(received)
    routed = jnp.take(stacked, (me - jnp.arange(groups, dtype=jnp.int32)) % groups, axis=0)
    return routed.reshape(1, 1, slot_count, local_cols)


def solution(mesh):
    in_specs = (
        P("section", "dp", None, "tensor"),
        P("section", "dp", None, None),
        P("section", "dp"),
        P("section", "dp"),
        P("section", "tensor"),
        P("section", "tensor", None),
    )
    out_specs = P("section", "dp", None, "tensor")
    return jax.shard_map(
        per_device, mesh=mesh, in_specs=in_specs, out_specs=out_specs, check_vma=False
    )
```

```python
import jax
import jax.numpy as jnp
from jax import lax
from jax.sharding import PartitionSpec as P

D = 16384
HD = 128


EPSILON = 1e-05
ROPE_BASE = 500000.0
CHUNK_EIGHTHS = (2, 2, 2, 2)


def shifted(block, axis, distance):
    devices = range(lax.axis_size(axis))
    route = [(i - distance, i) for i in devices if i - distance in devices]
    return lax.ppermute(block, axis, route)


def scatter_sum(keep, send, axis):
    size = lax.axis_size(axis)
    bit = 1
    while True:
        if bit >= 2:
            send = send.astype(jnp.bfloat16)
        pairs = [(i, i ^ bit) for i in range(size)]
        current = keep + lax.ppermute(send, axis, pairs).astype(jnp.float32)
        bit *= 2
        if bit >= size:
            return current[0]
        half = current.shape[0] // 2
        keep, send = current[:half], current[half:]


def all_sum(value, axis):
    size = lax.axis_size(axis)
    bit = 1
    while bit < size:
        value = value + lax.ppermute(value, axis, [(i, i ^ bit) for i in range(size)])
        bit *= 2
    return value


def bit_reversed(index, levels):
    return int(format(index, "0%db" % levels)[::-1], 2) if levels else 0


def rotate_keys(kv_cols, positions):
    head_size = kv_cols.shape[2]
    half_size = head_size // 2
    inverse = ROPE_BASE ** (-(jnp.arange(half_size, dtype=jnp.float32) * 2.0 / head_size))
    angles = inverse[:, None] * positions.astype(jnp.float32)[None, :]
    cosines = jnp.cos(angles)[None]
    sines = jnp.sin(angles)[None]
    key_part = kv_cols[:, 0]
    front_half = key_part[:, :half_size]
    back_half = key_part[:, half_size:]
    rotated = jnp.concatenate(
        [front_half * cosines - back_half * sines, back_half * cosines + front_half * sines],
        axis=1,
    )
    return jnp.stack([rotated, kv_cols[:, 1]], axis=1)


def per_device(hidden, owner, start, live, norm_gain, w_kv):
    groups = lax.axis_size("dp")
    tok_count = hidden.shape[2]
    capacity = 3 * tok_count // (2 * groups)
    slot_count = capacity * groups

    tok_rows = hidden[0, 0]
    target = owner[0, 0, :, 0]
    row_index = jnp.arange(tok_count, dtype=jnp.int32)
    row_alive = row_index < live[0, 0]
    onehot = (
        (target[:, None] == jnp.arange(groups, dtype=jnp.int32)[None, :]) & row_alive[:, None]
    ).astype(jnp.int32)
    row_rank = jnp.sum((jnp.cumsum(onehot, axis=0) - onehot) * onehot, axis=1)
    row_slot = jnp.where(row_alive, target * capacity + row_rank, slot_count)
    position = start[0, 0] + row_index
    widened = tok_rows.astype(jnp.float32)
    part_sq = jnp.sum(widened * widened, axis=1)
    meta = jnp.stack([part_sq, row_slot.astype(jnp.float32), position.astype(jnp.float32)])
    meta = shifted(meta, "section", 1)
    sum_sq = all_sum(meta[0], "tensor")

    first = lax.axis_index("section") == 0
    row_slot = jnp.where(first, slot_count, meta[1].astype(jnp.int32))
    position = meta[2].astype(jnp.int32)
    scale = lax.rsqrt(sum_sq / D + EPSILON)
    gain = norm_gain[0]
    weight = w_kv[0]
    local_width = tok_rows.shape[1]
    bounds = [local_width * sum(CHUNK_EIGHTHS[:k]) // 8 for k in range(len(CHUNK_EIGHTHS) + 1)]
    tensor = lax.axis_size("tensor")
    me_t = lax.axis_index("tensor")
    levels = tensor.bit_length() - 1
    block = weight.shape[1] // tensor
    partial = None
    for k in range(len(CHUNK_EIGHTHS)):
        cols = slice(bounds[k], bounds[k + 1])
        arrived = shifted(tok_rows[:, cols], "section", 1)
        if partial is not None:
            partial, arrived = lax.optimization_barrier((partial, arrived))
        normed = (arrived.astype(jnp.float32) * gain[cols] * scale[:, None]).astype(jnp.bfloat16)
        for low in range(bounds[k], bounds[k + 1], local_width // 8):
            part = slice(low, low + local_width // 8)
            sub = normed[:, low - bounds[k]:low - bounds[k] + local_width // 8]
            terms = []
            for s in range(tensor):
                column = jnp.bitwise_xor(me_t, bit_reversed(s, levels)) * block
                piece = lax.dynamic_slice_in_dim(weight[part], column, block, axis=1)
                terms.append(
                    lax.dot_general(
                        piece, sub, (((0,), (1,)), ((), ())), preferred_element_type=jnp.float32
                    )
                )
            term = (jnp.stack(terms[: tensor // 2]), jnp.stack(terms[tensor // 2:]))
            partial = term if partial is None else (partial[0] + term[0], partial[1] + term[1])
    summed = scatter_sum(partial[0], partial[1], "tensor")
    local_cols = summed.shape[0]
    local_kv = summed.reshape(local_cols // (2 * HD), 2, HD, tok_count)
    result = rotate_keys(local_kv, position).reshape(local_cols, tok_count).astype(jnp.bfloat16)

    placing = row_slot[None, :] == jnp.arange(slot_count, dtype=jnp.int32)[:, None]
    packed = lax.dot_general(
        placing.astype(jnp.bfloat16), result, (((1,), (1,)), ((), ())),
        preferred_element_type=jnp.float32,
    ).astype(jnp.bfloat16)
    packed = packed.reshape(groups, capacity, local_cols)
    me = lax.axis_index("dp")
    routed = jnp.zeros((groups, capacity, local_cols), jnp.bfloat16)
    routed = lax.dynamic_update_index_in_dim(
        routed, lax.dynamic_index_in_dim(packed, me, 0, keepdims=False), me, 0
    )
    for offset in range(1, groups):
        outgoing = lax.dynamic_index_in_dim(packed, (me + offset) % groups, 0, keepdims=False)
        pairs = [(i, (i + offset) % groups) for i in range(groups)]
        arrived = lax.ppermute(outgoing, "dp", pairs)
        routed = lax.dynamic_update_index_in_dim(routed, arrived, (me - offset) % groups, 0)
    return routed.reshape(1, 1, slot_count, local_cols)


def solution(mesh):
    in_specs = (
        P("section", "dp", None, "tensor"),
        P("section", "dp", None, None),
        P("section", "dp"),
        P("section", "dp"),
        P("section", "tensor"),
        P("section", "tensor", None),
    )
    out_specs = P("section", "dp", None, "tensor")
    return jax.shard_map(
        per_device, mesh=mesh, in_specs=in_specs, out_specs=out_specs, check_vma=False
    )
```

```python
import jax
import jax.numpy as jnp
from jax import lax
from jax.sharding import PartitionSpec as P

D = 16384
HD = 128


EPSILON = 1e-05
ROPE_BASE = 500000.0
CHUNK_EIGHTHS = (2, 2, 2, 2)


def shifted(block, axis, distance):
    devices = range(lax.axis_size(axis))
    route = [(i - distance, i) for i in devices if i - distance in devices]
    return lax.ppermute(block, axis, route)


def scatter_sum(blocks, axis):
    size = lax.axis_size(axis)
    current = blocks
    bit = 1
    while bit < size:
        half = current.shape[0] // 2
        keep, send = current[:half], current[half:]
        if bit >= 2:
            send = send.astype(jnp.bfloat16)
        pairs = [(i, i ^ bit) for i in range(size)]
        current = keep + lax.ppermute(send, axis, pairs).astype(jnp.float32)
        bit *= 2
    return current[0]


def all_sum(value, axis):
    size = lax.axis_size(axis)
    bit = 1
    while bit < size:
        value = value + lax.ppermute(value, axis, [(i, i ^ bit) for i in range(size)])
        bit *= 2
    return value


def bit_reversed(index, levels):
    return int(format(index, "0%db" % levels)[::-1], 2) if levels else 0


def rotate_keys(kv_cols, positions):
    head_size = kv_cols.shape[2]
    half_size = head_size // 2
    inverse = ROPE_BASE ** (-(jnp.arange(half_size, dtype=jnp.float32) * 2.0 / head_size))
    angles = inverse[:, None] * positions.astype(jnp.float32)[None, :]
    cosines = jnp.cos(angles)[None]
    sines = jnp.sin(angles)[None]
    key_part = kv_cols[:, 0]
    front_half = key_part[:, :half_size]
    back_half = key_part[:, half_size:]
    rotated = jnp.concatenate(
        [front_half * cosines - back_half * sines, back_half * cosines + front_half * sines],
        axis=1,
    )
    return jnp.stack([rotated, kv_cols[:, 1]], axis=1)


def per_device(hidden, owner, start, live, norm_gain, w_kv):
    groups = lax.axis_size("dp")
    tok_count = hidden.shape[2]
    capacity = 3 * tok_count // (2 * groups)
    slot_count = capacity * groups

    tok_rows = hidden[0, 0]
    target = owner[0, 0, :, 0]
    row_index = jnp.arange(tok_count, dtype=jnp.int32)
    row_alive = row_index < live[0, 0]
    onehot = (
        (target[:, None] == jnp.arange(groups, dtype=jnp.int32)[None, :]) & row_alive[:, None]
    ).astype(jnp.int32)
    row_rank = jnp.sum((jnp.cumsum(onehot, axis=0) - onehot) * onehot, axis=1)
    row_slot = jnp.where(row_alive, target * capacity + row_rank, slot_count)
    position = start[0, 0] + row_index
    widened = tok_rows.astype(jnp.float32)
    part_sq = jnp.sum(widened * widened, axis=1)
    meta = jnp.stack([part_sq, row_slot.astype(jnp.float32), position.astype(jnp.float32)])
    meta = shifted(meta, "section", 1)
    sum_sq = all_sum(meta[0], "tensor")

    first = lax.axis_index("section") == 0
    row_slot = jnp.where(first, slot_count, meta[1].astype(jnp.int32))
    position = meta[2].astype(jnp.int32)
    scale = lax.rsqrt(sum_sq / D + EPSILON)
    gain = norm_gain[0]
    weight = w_kv[0]
    local_width = tok_rows.shape[1]
    bounds = [local_width * sum(CHUNK_EIGHTHS[:k]) // 8 for k in range(len(CHUNK_EIGHTHS) + 1)]
    tensor = lax.axis_size("tensor")
    me_t = lax.axis_index("tensor")
    levels = tensor.bit_length() - 1
    block = weight.shape[1] // tensor
    partial = None
    for k in range(len(CHUNK_EIGHTHS)):
        cols = slice(bounds[k], bounds[k + 1])
        arrived = shifted(tok_rows[:, cols], "section", 1)
        if partial is not None:
            partial, arrived = lax.optimization_barrier((partial, arrived))
        normed = (arrived.astype(jnp.float32) * gain[cols] * scale[:, None]).astype(jnp.bfloat16)
        for low in range(bounds[k], bounds[k + 1], local_width // 8):
            part = slice(low, low + local_width // 8)
            sub = normed[:, low - bounds[k]:low - bounds[k] + local_width // 8]
            terms = []
            for s in range(tensor):
                column = jnp.bitwise_xor(me_t, bit_reversed(s, levels)) * block
                piece = lax.dynamic_slice_in_dim(weight[part], column, block, axis=1)
                terms.append(
                    lax.dot_general(
                        piece, sub, (((0,), (1,)), ((), ())), preferred_element_type=jnp.float32
                    )
                )
            term = jnp.stack(terms)
            partial = term if partial is None else partial + term
    summed = scatter_sum(partial, "tensor")
    local_cols = summed.shape[0]
    local_kv = summed.reshape(local_cols // (2 * HD), 2, HD, tok_count)
    result = rotate_keys(local_kv, position).reshape(local_cols, tok_count).astype(jnp.bfloat16)

    placing = row_slot[None, :] == jnp.arange(slot_count, dtype=jnp.int32)[:, None]
    packed = lax.dot_general(
        placing.astype(jnp.bfloat16), result, (((1,), (1,)), ((), ())),
        preferred_element_type=jnp.float32,
    ).astype(jnp.bfloat16)
    packed = packed.reshape(groups, capacity, local_cols)
    me = lax.axis_index("dp")
    routed = jnp.zeros((groups, capacity, local_cols), jnp.bfloat16)
    routed = lax.dynamic_update_index_in_dim(
        routed, lax.dynamic_index_in_dim(packed, me, 0, keepdims=False), me, 0
    )
    for offset in range(1, groups):
        outgoing = lax.dynamic_index_in_dim(packed, (me + offset) % groups, 0, keepdims=False)
        pairs = [(i, (i + offset) % groups) for i in range(groups)]
        arrived = lax.ppermute(outgoing, "dp", pairs)
        routed = lax.dynamic_update_index_in_dim(routed, arrived, (me - offset) % groups, 0)
    return routed.reshape(1, 1, slot_count, local_cols)


def solution(mesh):
    in_specs = (
        P("section", "dp", None, "tensor"),
        P("section", "dp", None, None),
        P("section", "dp"),
        P("section", "dp"),
        P("section", "tensor"),
        P("section", "tensor", None),
    )
    out_specs = P("section", "dp", None, "tensor")
    return jax.shard_map(
        per_device, mesh=mesh, in_specs=in_specs, out_specs=out_specs, check_vma=False
    )
```

```python
import jax
import jax.numpy as jnp
from jax import lax
from jax.sharding import PartitionSpec as P

D = 16384
HD = 128


EPSILON = 1e-05
ROPE_BASE = 500000.0
CHUNK_EIGHTHS = (3, 3, 2)


def shifted(block, axis, distance):
    devices = range(lax.axis_size(axis))
    route = [(i - distance, i) for i in devices if i - distance in devices]
    return lax.ppermute(block, axis, route)


def scatter_sum(blocks, axis):
    size = lax.axis_size(axis)
    current = blocks
    bit = 1
    while bit < size:
        half = current.shape[0] // 2
        keep, send = current[:half], current[half:]
        if bit >= 2:
            send = send.astype(jnp.bfloat16)
        pairs = [(i, i ^ bit) for i in range(size)]
        current = keep + lax.ppermute(send, axis, pairs).astype(jnp.float32)
        bit *= 2
    return current[0]


def all_sum(value, axis):
    size = lax.axis_size(axis)
    bit = 1
    while bit < size:
        value = value + lax.ppermute(value, axis, [(i, i ^ bit) for i in range(size)])
        bit *= 2
    return value


def bit_reversed(index, levels):
    return int(format(index, "0%db" % levels)[::-1], 2) if levels else 0


def rotate_keys(kv_cols, positions):
    head_size = kv_cols.shape[2]
    half_size = head_size // 2
    inverse = ROPE_BASE ** (-(jnp.arange(half_size, dtype=jnp.float32) * 2.0 / head_size))
    angles = inverse[:, None] * positions.astype(jnp.float32)[None, :]
    cosines = jnp.cos(angles)[None]
    sines = jnp.sin(angles)[None]
    key_part = kv_cols[:, 0]
    front_half = key_part[:, :half_size]
    back_half = key_part[:, half_size:]
    rotated = jnp.concatenate(
        [front_half * cosines - back_half * sines, back_half * cosines + front_half * sines],
        axis=1,
    )
    return jnp.stack([rotated, kv_cols[:, 1]], axis=1)


def per_device(hidden, owner, start, live, norm_gain, w_kv):
    groups = lax.axis_size("dp")
    tok_count = hidden.shape[2]
    capacity = 3 * tok_count // (2 * groups)
    slot_count = capacity * groups

    tok_rows = hidden[0, 0]
    target = owner[0, 0, :, 0]
    row_index = jnp.arange(tok_count, dtype=jnp.int32)
    row_alive = row_index < live[0, 0]
    onehot = (
        (target[:, None] == jnp.arange(groups, dtype=jnp.int32)[None, :]) & row_alive[:, None]
    ).astype(jnp.int32)
    row_rank = jnp.sum((jnp.cumsum(onehot, axis=0) - onehot) * onehot, axis=1)
    row_slot = jnp.where(row_alive, target * capacity + row_rank, slot_count)
    position = start[0, 0] + row_index
    widened = tok_rows.astype(jnp.float32)
    part_sq = jnp.sum(widened * widened, axis=1)
    meta = jnp.stack([part_sq, row_slot.astype(jnp.float32), position.astype(jnp.float32)])
    meta = shifted(meta, "section", 1)
    sum_sq = all_sum(meta[0], "tensor")

    first = lax.axis_index("section") == 0
    row_slot = jnp.where(first, slot_count, meta[1].astype(jnp.int32))
    position = meta[2].astype(jnp.int32)
    scale = lax.rsqrt(sum_sq / D + EPSILON)
    gain = norm_gain[0]
    weight = w_kv[0]
    local_width = tok_rows.shape[1]
    bounds = [local_width * sum(CHUNK_EIGHTHS[:k]) // 8 for k in range(len(CHUNK_EIGHTHS) + 1)]
    tensor = lax.axis_size("tensor")
    me_t = lax.axis_index("tensor")
    levels = tensor.bit_length() - 1
    block = weight.shape[1] // tensor
    partial = None
    for k in range(len(CHUNK_EIGHTHS)):
        cols = slice(bounds[k], bounds[k + 1])
        arrived = shifted(tok_rows[:, cols], "section", 1)
        if partial is not None:
            partial, arrived = lax.optimization_barrier((partial, arrived))
        normed = (arrived.astype(jnp.float32) * gain[cols] * scale[:, None]).astype(jnp.bfloat16)
        for low in range(bounds[k], bounds[k + 1], local_width // 8):
            part = slice(low, low + local_width // 8)
            sub = normed[:, low - bounds[k]:low - bounds[k] + local_width // 8]
            terms = []
            for s in range(tensor):
                column = jnp.bitwise_xor(me_t, bit_reversed(s, levels)) * block
                piece = lax.dynamic_slice_in_dim(weight[part], column, block, axis=1)
                terms.append(
                    lax.dot_general(
                        piece, sub, (((0,), (1,)), ((), ())), preferred_element_type=jnp.float32
                    )
                )
            term = jnp.stack(terms)
            partial = term if partial is None else partial + term
    summed = scatter_sum(partial, "tensor")
    local_cols = summed.shape[0]
    local_kv = summed.reshape(local_cols // (2 * HD), 2, HD, tok_count)
    result = rotate_keys(local_kv, position).reshape(local_cols, tok_count).astype(jnp.bfloat16)

    placing = row_slot[None, :] == jnp.arange(slot_count, dtype=jnp.int32)[:, None]
    packed = lax.dot_general(
        placing.astype(jnp.bfloat16), result, (((1,), (1,)), ((), ())),
        preferred_element_type=jnp.float32,
    ).astype(jnp.bfloat16)
    packed = packed.reshape(groups, capacity, local_cols)
    me = lax.axis_index("dp")
    routed = jnp.zeros((groups, capacity, local_cols), jnp.bfloat16)
    routed = lax.dynamic_update_index_in_dim(
        routed, lax.dynamic_index_in_dim(packed, me, 0, keepdims=False), me, 0
    )
    for offset in range(1, groups):
        outgoing = lax.dynamic_index_in_dim(packed, (me + offset) % groups, 0, keepdims=False)
        pairs = [(i, (i + offset) % groups) for i in range(groups)]
        arrived = lax.ppermute(outgoing, "dp", pairs)
        routed = lax.dynamic_update_index_in_dim(routed, arrived, (me - offset) % groups, 0)
    return routed.reshape(1, 1, slot_count, local_cols)


def solution(mesh):
    in_specs = (
        P("section", "dp", None, "tensor"),
        P("section", "dp", None, None),
        P("section", "dp"),
        P("section", "dp"),
        P("section", "tensor"),
        P("section", "tensor", None),
    )
    out_specs = P("section", "dp", None, "tensor")
    return jax.shard_map(
        per_device, mesh=mesh, in_specs=in_specs, out_specs=out_specs, check_vma=False
    )
```

```python
import jax
import jax.numpy as jnp
from jax import lax
from jax.sharding import PartitionSpec as P

D = 16384
HD = 128


EPSILON = 1e-05
ROPE_BASE = 500000.0
CHUNK_EIGHTHS = (6, 2)


def shifted(block, axis, distance):
    devices = range(lax.axis_size(axis))
    route = [(i - distance, i) for i in devices if i - distance in devices]
    return lax.ppermute(block, axis, route)


def scatter_sum(blocks, axis):
    size = lax.axis_size(axis)
    current = blocks
    bit = 1
    while bit < size:
        half = current.shape[0] // 2
        keep, send = current[:half], current[half:]
        if bit >= 2:
            send = send.astype(jnp.bfloat16)
        pairs = [(i, i ^ bit) for i in range(size)]
        current = keep + lax.ppermute(send, axis, pairs).astype(jnp.float32)
        bit *= 2
    return current[0]


def all_sum(value, axis):
    size = lax.axis_size(axis)
    bit = 1
    while bit < size:
        value = value + lax.ppermute(value, axis, [(i, i ^ bit) for i in range(size)])
        bit *= 2
    return value


def bit_reversed(index, levels):
    return int(format(index, "0%db" % levels)[::-1], 2) if levels else 0


def rotate_keys(kv_cols, positions):
    head_size = kv_cols.shape[2]
    half_size = head_size // 2
    inverse = ROPE_BASE ** (-(jnp.arange(half_size, dtype=jnp.float32) * 2.0 / head_size))
    angles = inverse[:, None] * positions.astype(jnp.float32)[None, :]
    cosines = jnp.cos(angles)[None]
    sines = jnp.sin(angles)[None]
    key_part = kv_cols[:, 0]
    front_half = key_part[:, :half_size]
    back_half = key_part[:, half_size:]
    rotated = jnp.concatenate(
        [front_half * cosines - back_half * sines, back_half * cosines + front_half * sines],
        axis=1,
    )
    return jnp.stack([rotated, kv_cols[:, 1]], axis=1)


def per_device(hidden, owner, start, live, norm_gain, w_kv):
    groups = lax.axis_size("dp")
    tok_count = hidden.shape[2]
    capacity = 3 * tok_count // (2 * groups)
    slot_count = capacity * groups

    tok_rows = hidden[0, 0]
    target = owner[0, 0, :, 0]
    row_index = jnp.arange(tok_count, dtype=jnp.int32)
    row_alive = row_index < live[0, 0]
    onehot = (
        (target[:, None] == jnp.arange(groups, dtype=jnp.int32)[None, :]) & row_alive[:, None]
    ).astype(jnp.int32)
    row_rank = jnp.sum((jnp.cumsum(onehot, axis=0) - onehot) * onehot, axis=1)
    row_slot = jnp.where(row_alive, target * capacity + row_rank, slot_count)
    position = start[0, 0] + row_index
    widened = tok_rows.astype(jnp.float32)
    part_sq = jnp.sum(widened * widened, axis=1)
    meta = jnp.stack([part_sq, row_slot.astype(jnp.float32), position.astype(jnp.float32)])
    meta = shifted(meta, "section", 1)
    sum_sq = all_sum(meta[0], "tensor")

    first = lax.axis_index("section") == 0
    row_slot = jnp.where(first, slot_count, meta[1].astype(jnp.int32))
    position = meta[2].astype(jnp.int32)
    scale = lax.rsqrt(sum_sq / D + EPSILON)
    gain = norm_gain[0]
    weight = w_kv[0]
    local_width = tok_rows.shape[1]
    bounds = [local_width * sum(CHUNK_EIGHTHS[:k]) // 8 for k in range(len(CHUNK_EIGHTHS) + 1)]
    tensor = lax.axis_size("tensor")
    me_t = lax.axis_index("tensor")
    levels = tensor.bit_length() - 1
    block = weight.shape[1] // tensor
    partial = None
    for k in range(len(CHUNK_EIGHTHS)):
        cols = slice(bounds[k], bounds[k + 1])
        arrived = shifted(tok_rows[:, cols], "section", 1)
        if partial is not None:
            partial, arrived = lax.optimization_barrier((partial, arrived))
        normed = (arrived.astype(jnp.float32) * gain[cols] * scale[:, None]).astype(jnp.bfloat16)
        for low in range(bounds[k], bounds[k + 1], local_width // 8):
            part = slice(low, low + local_width // 8)
            sub = normed[:, low - bounds[k]:low - bounds[k] + local_width // 8]
            terms = []
            for s in range(tensor):
                column = jnp.bitwise_xor(me_t, bit_reversed(s, levels)) * block
                piece = lax.dynamic_slice_in_dim(weight[part], column, block, axis=1)
                terms.append(
                    lax.dot_general(
                        piece, sub, (((0,), (1,)), ((), ())), preferred_element_type=jnp.float32
                    )
                )
            term = jnp.stack(terms)
            partial = term if partial is None else partial + term
    summed = scatter_sum(partial, "tensor")
    local_cols = summed.shape[0]
    local_kv = summed.reshape(local_cols // (2 * HD), 2, HD, tok_count)
    result = rotate_keys(local_kv, position).reshape(local_cols, tok_count).astype(jnp.bfloat16)

    placing = row_slot[None, :] == jnp.arange(slot_count, dtype=jnp.int32)[:, None]
    packed = lax.dot_general(
        placing.astype(jnp.bfloat16), result, (((1,), (1,)), ((), ())),
        preferred_element_type=jnp.float32,
    ).astype(jnp.bfloat16)
    packed = packed.reshape(groups, capacity, local_cols)
    me = lax.axis_index("dp")
    routed = jnp.zeros((groups, capacity, local_cols), jnp.bfloat16)
    routed = lax.dynamic_update_index_in_dim(
        routed, lax.dynamic_index_in_dim(packed, me, 0, keepdims=False), me, 0
    )
    for offset in range(1, groups):
        outgoing = lax.dynamic_index_in_dim(packed, (me + offset) % groups, 0, keepdims=False)
        pairs = [(i, (i + offset) % groups) for i in range(groups)]
        arrived = lax.ppermute(outgoing, "dp", pairs)
        routed = lax.dynamic_update_index_in_dim(routed, arrived, (me - offset) % groups, 0)
    return routed.reshape(1, 1, slot_count, local_cols)


def solution(mesh):
    in_specs = (
        P("section", "dp", None, "tensor"),
        P("section", "dp", None, None),
        P("section", "dp"),
        P("section", "dp"),
        P("section", "tensor"),
        P("section", "tensor", None),
    )
    out_specs = P("section", "dp", None, "tensor")
    return jax.shard_map(
        per_device, mesh=mesh, in_specs=in_specs, out_specs=out_specs, check_vma=False
    )
```

```python
import jax
import jax.numpy as jnp
from jax import lax
from jax.sharding import PartitionSpec as P

D = 16384
HD = 128


EPSILON = 1e-05
ROPE_BASE = 500000.0
CHUNK_EIGHTHS = (4, 3, 1)


def shifted(block, axis, distance):
    devices = range(lax.axis_size(axis))
    route = [(i - distance, i) for i in devices if i - distance in devices]
    return lax.ppermute(block, axis, route)


def scatter_sum(blocks, axis):
    size = lax.axis_size(axis)
    current = blocks
    bit = 1
    while bit < size:
        half = current.shape[0] // 2
        keep, send = current[:half], current[half:]
        if bit >= 2:
            send = send.astype(jnp.bfloat16)
        pairs = [(i, i ^ bit) for i in range(size)]
        current = keep + lax.ppermute(send, axis, pairs).astype(jnp.float32)
        bit *= 2
    return current[0]


def all_sum(value, axis):
    size = lax.axis_size(axis)
    bit = 1
    while bit < size:
        value = value + lax.ppermute(value, axis, [(i, i ^ bit) for i in range(size)])
        bit *= 2
    return value


def bit_reversed(index, levels):
    return int(format(index, "0%db" % levels)[::-1], 2) if levels else 0


def rotate_keys(kv_cols, positions):
    head_size = kv_cols.shape[2]
    half_size = head_size // 2
    inverse = ROPE_BASE ** (-(jnp.arange(half_size, dtype=jnp.float32) * 2.0 / head_size))
    angles = inverse[:, None] * positions.astype(jnp.float32)[None, :]
    cosines = jnp.cos(angles)[None]
    sines = jnp.sin(angles)[None]
    key_part = kv_cols[:, 0]
    front_half = key_part[:, :half_size]
    back_half = key_part[:, half_size:]
    rotated = jnp.concatenate(
        [front_half * cosines - back_half * sines, back_half * cosines + front_half * sines],
        axis=1,
    )
    return jnp.stack([rotated, kv_cols[:, 1]], axis=1)


def per_device(hidden, owner, start, live, norm_gain, w_kv):
    groups = lax.axis_size("dp")
    tok_count = hidden.shape[2]
    capacity = 3 * tok_count // (2 * groups)
    slot_count = capacity * groups

    tok_rows = hidden[0, 0]
    target = owner[0, 0, :, 0]
    row_index = jnp.arange(tok_count, dtype=jnp.int32)
    row_alive = row_index < live[0, 0]
    onehot = (
        (target[:, None] == jnp.arange(groups, dtype=jnp.int32)[None, :]) & row_alive[:, None]
    ).astype(jnp.int32)
    row_rank = jnp.sum((jnp.cumsum(onehot, axis=0) - onehot) * onehot, axis=1)
    row_slot = jnp.where(row_alive, target * capacity + row_rank, slot_count)
    position = start[0, 0] + row_index
    widened = tok_rows.astype(jnp.float32)
    part_sq = jnp.sum(widened * widened, axis=1)
    meta = jnp.stack([part_sq, row_slot.astype(jnp.float32), position.astype(jnp.float32)])
    meta = shifted(meta, "section", 1)
    sum_sq = all_sum(meta[0], "tensor")

    first = lax.axis_index("section") == 0
    row_slot = jnp.where(first, slot_count, meta[1].astype(jnp.int32))
    position = meta[2].astype(jnp.int32)
    scale = lax.rsqrt(sum_sq / D + EPSILON)
    gain = norm_gain[0]
    weight = w_kv[0]
    local_width = tok_rows.shape[1]
    bounds = [local_width * sum(CHUNK_EIGHTHS[:k]) // 8 for k in range(len(CHUNK_EIGHTHS) + 1)]
    tensor = lax.axis_size("tensor")
    me_t = lax.axis_index("tensor")
    levels = tensor.bit_length() - 1
    block = weight.shape[1] // tensor
    partial = None
    for k in range(len(CHUNK_EIGHTHS)):
        cols = slice(bounds[k], bounds[k + 1])
        arrived = shifted(tok_rows[:, cols], "section", 1)
        if partial is not None:
            partial, arrived = lax.optimization_barrier((partial, arrived))
        normed = (arrived.astype(jnp.float32) * gain[cols] * scale[:, None]).astype(jnp.bfloat16)
        for low in range(bounds[k], bounds[k + 1], local_width // 8):
            part = slice(low, low + local_width // 8)
            sub = normed[:, low - bounds[k]:low - bounds[k] + local_width // 8]
            terms = []
            for s in range(tensor):
                column = jnp.bitwise_xor(me_t, bit_reversed(s, levels)) * block
                piece = lax.dynamic_slice_in_dim(weight[part], column, block, axis=1)
                terms.append(
                    lax.dot_general(
                        piece, sub, (((0,), (1,)), ((), ())), preferred_element_type=jnp.float32
                    )
                )
            term = jnp.stack(terms)
            partial = term if partial is None else partial + term
    summed = scatter_sum(partial, "tensor")
    local_cols = summed.shape[0]
    local_kv = summed.reshape(local_cols // (2 * HD), 2, HD, tok_count)
    result = rotate_keys(local_kv, position).reshape(local_cols, tok_count).astype(jnp.bfloat16)

    placing = row_slot[None, :] == jnp.arange(slot_count, dtype=jnp.int32)[:, None]
    packed = lax.dot_general(
        placing.astype(jnp.bfloat16), result, (((1,), (1,)), ((), ())),
        preferred_element_type=jnp.float32,
    ).astype(jnp.bfloat16)
    packed = packed.reshape(groups, capacity, local_cols)
    me = lax.axis_index("dp")
    routed = jnp.zeros((groups, capacity, local_cols), jnp.bfloat16)
    routed = lax.dynamic_update_index_in_dim(
        routed, lax.dynamic_index_in_dim(packed, me, 0, keepdims=False), me, 0
    )
    for offset in range(1, groups):
        outgoing = lax.dynamic_index_in_dim(packed, (me + offset) % groups, 0, keepdims=False)
        pairs = [(i, (i + offset) % groups) for i in range(groups)]
        arrived = lax.ppermute(outgoing, "dp", pairs)
        routed = lax.dynamic_update_index_in_dim(routed, arrived, (me - offset) % groups, 0)
    return routed.reshape(1, 1, slot_count, local_cols)


def solution(mesh):
    in_specs = (
        P("section", "dp", None, "tensor"),
        P("section", "dp", None, None),
        P("section", "dp"),
        P("section", "dp"),
        P("section", "tensor"),
        P("section", "tensor", None),
    )
    out_specs = P("section", "dp", None, "tensor")
    return jax.shard_map(
        per_device, mesh=mesh, in_specs=in_specs, out_specs=out_specs, check_vma=False
    )
```

```python
import jax
import jax.numpy as jnp
from jax import lax
from jax.sharding import PartitionSpec as P

D = 16384
HD = 128


EPSILON = 1e-05
ROPE_BASE = 500000.0
CHUNK_EIGHTHS = (5, 2, 1)


def shifted(block, axis, distance):
    devices = range(lax.axis_size(axis))
    route = [(i - distance, i) for i in devices if i - distance in devices]
    return lax.ppermute(block, axis, route)


def scatter_sum(blocks, axis):
    size = lax.axis_size(axis)
    current = blocks
    bit = 1
    while bit < size:
        half = current.shape[0] // 2
        keep, send = current[:half], current[half:]
        if bit >= 2:
            send = send.astype(jnp.bfloat16)
        pairs = [(i, i ^ bit) for i in range(size)]
        current = keep + lax.ppermute(send, axis, pairs).astype(jnp.float32)
        bit *= 2
    return current[0]


def all_sum(value, axis):
    size = lax.axis_size(axis)
    bit = 1
    while bit < size:
        value = value + lax.ppermute(value, axis, [(i, i ^ bit) for i in range(size)])
        bit *= 2
    return value


def bit_reversed(index, levels):
    return int(format(index, "0%db" % levels)[::-1], 2) if levels else 0


def rotate_keys(kv_cols, positions):
    head_size = kv_cols.shape[2]
    half_size = head_size // 2
    inverse = ROPE_BASE ** (-(jnp.arange(half_size, dtype=jnp.float32) * 2.0 / head_size))
    angles = inverse[:, None] * positions.astype(jnp.float32)[None, :]
    cosines = jnp.cos(angles)[None]
    sines = jnp.sin(angles)[None]
    key_part = kv_cols[:, 0]
    front_half = key_part[:, :half_size]
    back_half = key_part[:, half_size:]
    rotated = jnp.concatenate(
        [front_half * cosines - back_half * sines, back_half * cosines + front_half * sines],
        axis=1,
    )
    return jnp.stack([rotated, kv_cols[:, 1]], axis=1)


def per_device(hidden, owner, start, live, norm_gain, w_kv):
    groups = lax.axis_size("dp")
    tok_count = hidden.shape[2]
    capacity = 3 * tok_count // (2 * groups)
    slot_count = capacity * groups

    tok_rows = hidden[0, 0]
    target = owner[0, 0, :, 0]
    row_index = jnp.arange(tok_count, dtype=jnp.int32)
    row_alive = row_index < live[0, 0]
    onehot = (
        (target[:, None] == jnp.arange(groups, dtype=jnp.int32)[None, :]) & row_alive[:, None]
    ).astype(jnp.int32)
    row_rank = jnp.sum((jnp.cumsum(onehot, axis=0) - onehot) * onehot, axis=1)
    row_slot = jnp.where(row_alive, target * capacity + row_rank, slot_count)
    position = start[0, 0] + row_index
    widened = tok_rows.astype(jnp.float32)
    part_sq = jnp.sum(widened * widened, axis=1)
    meta = jnp.stack([part_sq, row_slot.astype(jnp.float32), position.astype(jnp.float32)])
    meta = shifted(meta, "section", 1)
    sum_sq = all_sum(meta[0], "tensor")

    first = lax.axis_index("section") == 0
    row_slot = jnp.where(first, slot_count, meta[1].astype(jnp.int32))
    position = meta[2].astype(jnp.int32)
    scale = lax.rsqrt(sum_sq / D + EPSILON)
    gain = norm_gain[0]
    weight = w_kv[0]
    local_width = tok_rows.shape[1]
    bounds = [local_width * sum(CHUNK_EIGHTHS[:k]) // 8 for k in range(len(CHUNK_EIGHTHS) + 1)]
    tensor = lax.axis_size("tensor")
    me_t = lax.axis_index("tensor")
    levels = tensor.bit_length() - 1
    block = weight.shape[1] // tensor
    partial = None
    for k in range(len(CHUNK_EIGHTHS)):
        cols = slice(bounds[k], bounds[k + 1])
        arrived = shifted(tok_rows[:, cols], "section", 1)
        if partial is not None:
            partial, arrived = lax.optimization_barrier((partial, arrived))
        normed = (arrived.astype(jnp.float32) * gain[cols] * scale[:, None]).astype(jnp.bfloat16)
        for low in range(bounds[k], bounds[k + 1], local_width // 8):
            part = slice(low, low + local_width // 8)
            sub = normed[:, low - bounds[k]:low - bounds[k] + local_width // 8]
            terms = []
            for s in range(tensor):
                column = jnp.bitwise_xor(me_t, bit_reversed(s, levels)) * block
                piece = lax.dynamic_slice_in_dim(weight[part], column, block, axis=1)
                terms.append(
                    lax.dot_general(
                        piece, sub, (((0,), (1,)), ((), ())), preferred_element_type=jnp.float32
                    )
                )
            term = jnp.stack(terms)
            partial = term if partial is None else partial + term
    summed = scatter_sum(partial, "tensor")
    local_cols = summed.shape[0]
    local_kv = summed.reshape(local_cols // (2 * HD), 2, HD, tok_count)
    result = rotate_keys(local_kv, position).reshape(local_cols, tok_count).astype(jnp.bfloat16)

    placing = row_slot[None, :] == jnp.arange(slot_count, dtype=jnp.int32)[:, None]
    packed = lax.dot_general(
        placing.astype(jnp.bfloat16), result, (((1,), (1,)), ((), ())),
        preferred_element_type=jnp.float32,
    ).astype(jnp.bfloat16)
    packed = packed.reshape(groups, capacity, local_cols)
    me = lax.axis_index("dp")
    routed = jnp.zeros((groups, capacity, local_cols), jnp.bfloat16)
    routed = lax.dynamic_update_index_in_dim(
        routed, lax.dynamic_index_in_dim(packed, me, 0, keepdims=False), me, 0
    )
    for offset in range(1, groups):
        outgoing = lax.dynamic_index_in_dim(packed, (me + offset) % groups, 0, keepdims=False)
        pairs = [(i, (i + offset) % groups) for i in range(groups)]
        arrived = lax.ppermute(outgoing, "dp", pairs)
        routed = lax.dynamic_update_index_in_dim(routed, arrived, (me - offset) % groups, 0)
    return routed.reshape(1, 1, slot_count, local_cols)


def solution(mesh):
    in_specs = (
        P("section", "dp", None, "tensor"),
        P("section", "dp", None, None),
        P("section", "dp"),
        P("section", "dp"),
        P("section", "tensor"),
        P("section", "tensor", None),
    )
    out_specs = P("section", "dp", None, "tensor")
    return jax.shard_map(
        per_device, mesh=mesh, in_specs=in_specs, out_specs=out_specs, check_vma=False
    )
```

```python
import jax
import jax.numpy as jnp
from jax import lax
from jax.sharding import PartitionSpec as P

D = 16384
HD = 128


EPSILON = 1e-05
ROPE_BASE = 500000.0
CHUNK_EIGHTHS = (4, 2, 2)


def shifted(block, axis, distance):
    devices = range(lax.axis_size(axis))
    route = [(i - distance, i) for i in devices if i - distance in devices]
    return lax.ppermute(block, axis, route)


def scatter_sum(blocks, axis):
    size = lax.axis_size(axis)
    current = blocks
    bit = 1
    while bit < size:
        half = current.shape[0] // 2
        keep, send = current[:half], current[half:]
        if bit >= 2:
            send = send.astype(jnp.bfloat16)
        pairs = [(i, i ^ bit) for i in range(size)]
        current = keep + lax.ppermute(send, axis, pairs).astype(jnp.float32)
        bit *= 2
    return current[0]


def all_sum(value, axis):
    size = lax.axis_size(axis)
    bit = 1
    while bit < size:
        value = value + lax.ppermute(value, axis, [(i, i ^ bit) for i in range(size)])
        bit *= 2
    return value


def bit_reversed(index, levels):
    return int(format(index, "0%db" % levels)[::-1], 2) if levels else 0


def rotate_keys(kv_cols, positions):
    head_size = kv_cols.shape[2]
    half_size = head_size // 2
    inverse = ROPE_BASE ** (-(jnp.arange(half_size, dtype=jnp.float32) * 2.0 / head_size))
    angles = inverse[:, None] * positions.astype(jnp.float32)[None, :]
    cosines = jnp.cos(angles)[None]
    sines = jnp.sin(angles)[None]
    key_part = kv_cols[:, 0]
    front_half = key_part[:, :half_size]
    back_half = key_part[:, half_size:]
    rotated = jnp.concatenate(
        [front_half * cosines - back_half * sines, back_half * cosines + front_half * sines],
        axis=1,
    )
    return jnp.stack([rotated, kv_cols[:, 1]], axis=1)


def per_device(hidden, owner, start, live, norm_gain, w_kv):
    groups = lax.axis_size("dp")
    tok_count = hidden.shape[2]
    capacity = 3 * tok_count // (2 * groups)
    slot_count = capacity * groups

    tok_rows = hidden[0, 0]
    target = owner[0, 0, :, 0]
    row_index = jnp.arange(tok_count, dtype=jnp.int32)
    row_alive = row_index < live[0, 0]
    onehot = (
        (target[:, None] == jnp.arange(groups, dtype=jnp.int32)[None, :]) & row_alive[:, None]
    ).astype(jnp.int32)
    row_rank = jnp.sum((jnp.cumsum(onehot, axis=0) - onehot) * onehot, axis=1)
    row_slot = jnp.where(row_alive, target * capacity + row_rank, slot_count)
    position = start[0, 0] + row_index
    widened = tok_rows.astype(jnp.float32)
    part_sq = jnp.sum(widened * widened, axis=1)
    meta = jnp.stack([part_sq, row_slot.astype(jnp.float32), position.astype(jnp.float32)])
    meta = shifted(meta, "section", 1)
    sum_sq = all_sum(meta[0], "tensor")

    first = lax.axis_index("section") == 0
    row_slot = jnp.where(first, slot_count, meta[1].astype(jnp.int32))
    position = meta[2].astype(jnp.int32)
    scale = lax.rsqrt(sum_sq / D + EPSILON)
    gain = norm_gain[0]
    weight = w_kv[0]
    local_width = tok_rows.shape[1]
    bounds = [local_width * sum(CHUNK_EIGHTHS[:k]) // 8 for k in range(len(CHUNK_EIGHTHS) + 1)]
    tensor = lax.axis_size("tensor")
    me_t = lax.axis_index("tensor")
    levels = tensor.bit_length() - 1
    block = weight.shape[1] // tensor
    partial = None
    for k in range(len(CHUNK_EIGHTHS)):
        cols = slice(bounds[k], bounds[k + 1])
        arrived = shifted(tok_rows[:, cols], "section", 1)
        if partial is not None:
            partial, arrived = lax.optimization_barrier((partial, arrived))
        normed = (arrived.astype(jnp.float32) * gain[cols] * scale[:, None]).astype(jnp.bfloat16)
        for low in range(bounds[k], bounds[k + 1], local_width // 8):
            part = slice(low, low + local_width // 8)
            sub = normed[:, low - bounds[k]:low - bounds[k] + local_width // 8]
            terms = []
            for s in range(tensor):
                column = jnp.bitwise_xor(me_t, bit_reversed(s, levels)) * block
                piece = lax.dynamic_slice_in_dim(weight[part], column, block, axis=1)
                terms.append(
                    lax.dot_general(
                        piece, sub, (((0,), (1,)), ((), ())), preferred_element_type=jnp.float32
                    )
                )
            term = jnp.stack(terms)
            partial = term if partial is None else partial + term
    summed = scatter_sum(partial, "tensor")
    local_cols = summed.shape[0]
    local_kv = summed.reshape(local_cols // (2 * HD), 2, HD, tok_count)
    result = rotate_keys(local_kv, position).reshape(local_cols, tok_count).astype(jnp.bfloat16)

    placing = row_slot[None, :] == jnp.arange(slot_count, dtype=jnp.int32)[:, None]
    packed = lax.dot_general(
        placing.astype(jnp.bfloat16), result, (((1,), (1,)), ((), ())),
        preferred_element_type=jnp.float32,
    ).astype(jnp.bfloat16)
    packed = packed.reshape(groups, capacity, local_cols)
    me = lax.axis_index("dp")
    routed = jnp.zeros((groups, capacity, local_cols), jnp.bfloat16)
    routed = lax.dynamic_update_index_in_dim(
        routed, lax.dynamic_index_in_dim(packed, me, 0, keepdims=False), me, 0
    )
    for offset in range(1, groups):
        outgoing = lax.dynamic_index_in_dim(packed, (me + offset) % groups, 0, keepdims=False)
        pairs = [(i, (i + offset) % groups) for i in range(groups)]
        arrived = lax.ppermute(outgoing, "dp", pairs)
        routed = lax.dynamic_update_index_in_dim(routed, arrived, (me - offset) % groups, 0)
    return routed.reshape(1, 1, slot_count, local_cols)


def solution(mesh):
    in_specs = (
        P("section", "dp", None, "tensor"),
        P("section", "dp", None, None),
        P("section", "dp"),
        P("section", "dp"),
        P("section", "tensor"),
        P("section", "tensor", None),
    )
    out_specs = P("section", "dp", None, "tensor")
    return jax.shard_map(
        per_device, mesh=mesh, in_specs=in_specs, out_specs=out_specs, check_vma=False
    )
```

```python
import jax
import jax.numpy as jnp
from jax import lax
from jax.sharding import PartitionSpec as P

D = 16384
HD = 128


EPSILON = 1e-05
ROPE_BASE = 500000.0
CHUNK_EIGHTHS = (3, 2, 2, 1)


def shifted(block, axis, distance):
    devices = range(lax.axis_size(axis))
    route = [(i - distance, i) for i in devices if i - distance in devices]
    return lax.ppermute(block, axis, route)


def scatter_sum(blocks, axis):
    size = lax.axis_size(axis)
    current = blocks
    bit = 1
    while bit < size:
        half = current.shape[0] // 2
        keep, send = current[:half], current[half:]
        if bit >= 2:
            send = send.astype(jnp.bfloat16)
        pairs = [(i, i ^ bit) for i in range(size)]
        current = keep + lax.ppermute(send, axis, pairs).astype(jnp.float32)
        bit *= 2
    return current[0]


def all_sum(value, axis):
    size = lax.axis_size(axis)
    bit = 1
    while bit < size:
        value = value + lax.ppermute(value, axis, [(i, i ^ bit) for i in range(size)])
        bit *= 2
    return value


def bit_reversed(index, levels):
    return int(format(index, "0%db" % levels)[::-1], 2) if levels else 0


def rotate_keys(kv_cols, positions):
    head_size = kv_cols.shape[2]
    half_size = head_size // 2
    inverse = ROPE_BASE ** (-(jnp.arange(half_size, dtype=jnp.float32) * 2.0 / head_size))
    angles = inverse[:, None] * positions.astype(jnp.float32)[None, :]
    cosines = jnp.cos(angles)[None]
    sines = jnp.sin(angles)[None]
    key_part = kv_cols[:, 0]
    front_half = key_part[:, :half_size]
    back_half = key_part[:, half_size:]
    rotated = jnp.concatenate(
        [front_half * cosines - back_half * sines, back_half * cosines + front_half * sines],
        axis=1,
    )
    return jnp.stack([rotated, kv_cols[:, 1]], axis=1)


def per_device(hidden, owner, start, live, norm_gain, w_kv):
    groups = lax.axis_size("dp")
    tok_count = hidden.shape[2]
    capacity = 3 * tok_count // (2 * groups)
    slot_count = capacity * groups

    tok_rows = hidden[0, 0]
    target = owner[0, 0, :, 0]
    row_index = jnp.arange(tok_count, dtype=jnp.int32)
    row_alive = row_index < live[0, 0]
    onehot = (
        (target[:, None] == jnp.arange(groups, dtype=jnp.int32)[None, :]) & row_alive[:, None]
    ).astype(jnp.int32)
    row_rank = jnp.sum((jnp.cumsum(onehot, axis=0) - onehot) * onehot, axis=1)
    row_slot = jnp.where(row_alive, target * capacity + row_rank, slot_count)
    position = start[0, 0] + row_index
    widened = tok_rows.astype(jnp.float32)
    part_sq = jnp.sum(widened * widened, axis=1)
    meta = jnp.stack([part_sq, row_slot.astype(jnp.float32), position.astype(jnp.float32)])
    meta = shifted(meta, "section", 1)
    sum_sq = all_sum(meta[0], "tensor")

    first = lax.axis_index("section") == 0
    row_slot = jnp.where(first, slot_count, meta[1].astype(jnp.int32))
    position = meta[2].astype(jnp.int32)
    scale = lax.rsqrt(sum_sq / D + EPSILON)
    gain = norm_gain[0]
    weight = w_kv[0]
    local_width = tok_rows.shape[1]
    bounds = [local_width * sum(CHUNK_EIGHTHS[:k]) // 8 for k in range(len(CHUNK_EIGHTHS) + 1)]
    tensor = lax.axis_size("tensor")
    me_t = lax.axis_index("tensor")
    levels = tensor.bit_length() - 1
    block = weight.shape[1] // tensor
    partial = None
    for k in range(len(CHUNK_EIGHTHS)):
        cols = slice(bounds[k], bounds[k + 1])
        arrived = shifted(tok_rows[:, cols], "section", 1)
        if partial is not None:
            partial, arrived = lax.optimization_barrier((partial, arrived))
        normed = (arrived.astype(jnp.float32) * gain[cols] * scale[:, None]).astype(jnp.bfloat16)
        for low in range(bounds[k], bounds[k + 1], local_width // 8):
            part = slice(low, low + local_width // 8)
            sub = normed[:, low - bounds[k]:low - bounds[k] + local_width // 8]
            terms = []
            for s in range(tensor):
                column = jnp.bitwise_xor(me_t, bit_reversed(s, levels)) * block
                piece = lax.dynamic_slice_in_dim(weight[part], column, block, axis=1)
                terms.append(
                    lax.dot_general(
                        piece, sub, (((0,), (1,)), ((), ())), preferred_element_type=jnp.float32
                    )
                )
            term = jnp.stack(terms)
            partial = term if partial is None else partial + term
    summed = scatter_sum(partial, "tensor")
    local_cols = summed.shape[0]
    local_kv = summed.reshape(local_cols // (2 * HD), 2, HD, tok_count)
    result = rotate_keys(local_kv, position).reshape(local_cols, tok_count).astype(jnp.bfloat16)

    placing = row_slot[None, :] == jnp.arange(slot_count, dtype=jnp.int32)[:, None]
    packed = lax.dot_general(
        placing.astype(jnp.bfloat16), result, (((1,), (1,)), ((), ())),
        preferred_element_type=jnp.float32,
    ).astype(jnp.bfloat16)
    packed = packed.reshape(groups, capacity, local_cols)
    me = lax.axis_index("dp")
    routed = jnp.zeros((groups, capacity, local_cols), jnp.bfloat16)
    routed = lax.dynamic_update_index_in_dim(
        routed, lax.dynamic_index_in_dim(packed, me, 0, keepdims=False), me, 0
    )
    for offset in range(1, groups):
        outgoing = lax.dynamic_index_in_dim(packed, (me + offset) % groups, 0, keepdims=False)
        pairs = [(i, (i + offset) % groups) for i in range(groups)]
        arrived = lax.ppermute(outgoing, "dp", pairs)
        routed = lax.dynamic_update_index_in_dim(routed, arrived, (me - offset) % groups, 0)
    return routed.reshape(1, 1, slot_count, local_cols)


def solution(mesh):
    in_specs = (
        P("section", "dp", None, "tensor"),
        P("section", "dp", None, None),
        P("section", "dp"),
        P("section", "dp"),
        P("section", "tensor"),
        P("section", "tensor", None),
    )
    out_specs = P("section", "dp", None, "tensor")
    return jax.shard_map(
        per_device, mesh=mesh, in_specs=in_specs, out_specs=out_specs, check_vma=False
    )
```
